32 devices in a mesh: vocab: 8 (over z, y), grp: 4 (over x, core).
Axes of the slice: x: 2, y: 2, z: 4, core: 2. Of those that a mesh axis runs over, the one named last changes fastest.
Arguments:
- states: bfloat16 [4, 96, 4096], P('grp', 'vocab'), may hold values from -256 to 256
- target_ids: int32 [4, 96], P('grp', 'vocab'), may hold values from 0 to 65535
- lengths: int32 [4, 8], P('grp'), may hold values from 1 to 12, 72 in all within a row
- order: int32 [4, 8], replicated, may hold values from 0 to 7, each once within a row
- gain: float32 [4096], replicated, may hold values from 0.25 to 1.75
- head: bfloat16 [4096, 65536], P(None, 'vocab'), may hold values from -16 to 16
Outputs:
- log_prob: float32 [4, 96], P('grp', 'vocab')
- entropy: float32 [4, 96], P('grp', 'vocab')
- state_norm: float32 [4, 96], P('grp', 'vocab')
- peak_logit: float32 [4, 96], P('grp', 'vocab')
The draws below stay inside these ranges and needn't reach their ends.
Inputs may be any that keep to these rules, and one draw needn't show every extreme that they name: `order`: each row is a permutation of 0 to 7. `lengths`: each row sums to 72.
All inputs are finite; a program needn't handle non-finite values.
Results may differ from the reference program's by a relative error of at most 0.011.
The reference program's roundings to bfloat16 on the way (of `normed`) count: a program that leaves them out, or rounds other values in their place, can miss the bound.
Values may be sent and summed in bfloat16 or wider, within the bound.
No kernel may reach another device: no remote copies, remote signals or barrier semaphores. Data moves between devices by JAX's collectives and lax.ppermute only.
A program may use at most 256 MiB of HBM per device.

```python
import math
from functools import partial
import jax
import jax.numpy as jnp
import numpy as np
from jax import lax

D = 4096
VOCAB = 65536
ROWS_DEV = 12
GROUP_ROWS = 96
N_VOCAB = 8
N_GRP = 4


def draw_states(key, part):
    key_base, key_row, key_col = jax.random.split(key, 3)
    base_values = jax.random.normal(key_base, (N_GRP, GROUP_ROWS, D), jnp.float32)
    scale_top = math.log(10.0)
    row_scale = jnp.exp(jax.random.uniform(key_row, (N_GRP, GROUP_ROWS, 1), jnp.float32, 0.0, scale_top))
    col_scale = jnp.exp(jax.random.uniform(key_col, (D,), jnp.float32, 0.0, math.log(10.0)))
    return jnp.clip(base_values * row_scale * col_scale, -256.0, 256.0).astype(jnp.bfloat16)


def draw_head(key, part):
    key_base = jax.random.fold_in(key, 0)
    base_values = jax.random.normal(key_base, (D, VOCAB), jnp.float32) * 0.05
    return jnp.clip(base_values, -16.0, 16.0).astype(jnp.bfloat16)


def place_ends(result, stream_key, low, largest):
    longest = result.shape.index(max(result.shape))
    spots = []
    for shift in (0, 1):
        where = [jax.random.randint(jax.random.fold_in(stream_key, axis), (), 0, length) for axis, length in enumerate(result.shape)]
        where[longest] = (where[longest] + shift) % result.shape[longest]
        spots.append(tuple(where))
    return result.at[spots[0]].set(low).at[spots[1]].set(largest)


def cumulative_ranks(number_of, lean):
    weights = [(1 << 20) // math.isqrt(grade ** lean) + 1 for grade in range(1, number_of + 1)]
    spread = 1 + sum(weights) // (1 << 30)
    return np.cumsum(np.array([max(1, weight // spread) for weight in weights]))


def ranked(stream_key, extent, amount, lean):
    grid = cumulative_ranks(amount, lean)
    pick = jax.random.randint(jax.random.fold_in(stream_key, 1), extent, 0, int(grid[amount - 1]))
    grade = jnp.searchsorted(jnp.asarray(grid, jnp.int32), pick, side="right")
    return jax.random.permutation(jax.random.fold_in(stream_key, 2), amount)[grade].astype(jnp.int32)


def length_profile(count, total, most, lean):
    portions = [(1 << 20) // math.isqrt(standing ** lean) + 1 for standing in range(2, count + 1)]
    rest, given = total - most - (count - 1), [1] * (count - 1)
    while rest > 0:
        free = [i for i in range(count - 1) if given[i] < most]
        whole, budget = sum([portions[i] for i in free]), rest
        for i in free:
            more = min(most - given[i], max(1, budget * portions[i] // whole), rest)
            given[i] = given[i] + more
            rest = rest - more
    return np.array([most] + given)


def uneven(own_key, amount, total, most, slope):
    if amount == 2:
        one = jax.random.randint(own_key, (), max(1, total - most), min(most, total - 1) + 1)
        return jnp.stack([one, total - one])
    tallies = jnp.asarray(length_profile(amount, total, most, slope), jnp.int32)
    pairs = (amount - 1) // 2
    giver, sink = tallies[1:1 + 2 * pairs:2], tallies[2:2 + 2 * pairs:2]
    margin = jnp.minimum(giver - 1, most - sink)
    passed = jax.random.randint(jax.random.fold_in(own_key, 1), (pairs,), 0, 1 << 20) % (margin + 1)
    tallies = tallies.at[1:1 + 2 * pairs:2].set(giver - passed).at[2:2 + 2 * pairs:2].set(sink + passed)
    return tallies[jax.random.permutation(jax.random.fold_in(own_key, 2), amount)]


def setup_inputs(seed: int = 0) -> dict:
    key_list = jax.random.split(jax.random.key(seed), 7)
    return {
        "states": draw_states(jax.random.fold_in(key_list[6], 71), 0),
        "target_ids": place_ends(ranked(key_list[1], (N_GRP, GROUP_ROWS), VOCAB, 2), jax.random.fold_in(key_list[1], 3), 0, VOCAB - 1).astype(jnp.int32),
        "lengths": jax.vmap(lambda own: uneven(own, N_VOCAB, N_VOCAB * ROWS_DEV * 3 // 4, ROWS_DEV, 1))(jax.random.split(key_list[2], N_GRP)).reshape((N_GRP, N_VOCAB)).astype(jnp.int32),
        "order": jax.vmap(lambda own: jax.random.permutation(own, N_VOCAB))(jax.random.split(key_list[3], N_GRP)).reshape((N_GRP, N_VOCAB)).astype(jnp.int32),
        "gain": jnp.clip(1.0 + 0.15 * jax.random.normal(key_list[4], (D,), jnp.float32), 0.25, 1.75),
        "head": draw_head(jax.random.fold_in(key_list[6], 71), 0),
    }


EPSILON = 1e-05

def score_group(gain, head, group_args):
    group_states, group_ids = group_args
    values = group_states.astype(jnp.float32)
    mean_square = lax.optimization_barrier(jnp.mean(values * values, axis=-1))
    normed = (values * lax.rsqrt(mean_square + EPSILON)[:, None] * gain).astype(jnp.bfloat16)
    logits = jnp.dot(normed, head, preferred_element_type=jnp.float32)
    peak = lax.optimization_barrier(jnp.max(logits, axis=1))
    weights = jnp.exp(logits - peak[:, None])
    totals = lax.optimization_barrier(jnp.sum(weights, axis=1))
    expected = lax.optimization_barrier(jnp.sum(weights * logits, axis=1))
    target_logit = jnp.take_along_axis(logits, group_ids[:, None].astype(jnp.int32), axis=1)[:, 0]
    log_total = jnp.log(totals)
    return jnp.stack([target_logit - peak - log_total, peak + log_total - expected / totals, jnp.sqrt(mean_square), peak])

def reference(states, target_ids, lengths, order, gain, head):
    results = lax.map(partial(score_group, gain, head), (states, target_ids))
    groups = results.shape[0]
    blocks = lengths.shape[1]
    results = results.reshape(groups, 4, blocks, ROWS_DEV)
    keep = (jnp.arange(ROWS_DEV, dtype=jnp.int32)[None, None, :] < lengths[:, :, None]).astype(results.dtype)
    results = results * keep[:, None]
    moved = results.transpose(0, 2, 1, 3)
    placed = jnp.zeros_like(moved).at[jnp.arange(groups, dtype=jnp.int32)[:, None], order].set(moved)
    placed = placed.transpose(2, 0, 1, 3).reshape(4, groups, blocks * ROWS_DEV)
    return (placed[0], placed[1], placed[2], placed[3])
```

```python
import jax
import jax.numpy as jnp
from jax import lax
from jax.sharding import PartitionSpec as P

EPSILON = 1e-05
RADIX = 256
LANES = 128


def digit_count(total):
    digits = 1
    while RADIX**digits < total:
        digits += 1
    return digits


def normalize(block_states, gain):
    values = block_states.astype(jnp.float32)
    mean_square = jnp.mean(values * values, axis=-1)
    normed = (values * lax.rsqrt(mean_square + EPSILON)[:, None] * gain).astype(jnp.bfloat16)
    return (normed, jnp.sqrt(mean_square))


def partial_stats(normed, columns, token_ids, offset):
    logits = jnp.dot(normed, columns, preferred_element_type=jnp.float32)
    local_max = jnp.max(logits, axis=1)
    weights = jnp.exp(logits - local_max[:, None])
    width = columns.shape[1]
    within = token_ids - offset
    inside = (within >= 0) & (within < width)
    picked = jnp.take_along_axis(logits, jnp.clip(within, 0, width - 1)[:, None], axis=1)[:, 0]
    return (
        local_max,
        jnp.sum(weights, axis=1),
        jnp.sum(weights * logits, axis=1),
        jnp.where(inside, picked, 0.0),
    )


def shards(states, target_ids, lengths, order, gain, head):
    count = states.shape[1]
    vocab_size = lax.axis_size("vocab")
    vocab_index = lax.axis_index("vocab")
    group_index = lax.axis_index("grp")
    own_order = lax.dynamic_index_in_dim(order, group_index, 0, keepdims=False)
    block_ids = jnp.arange(vocab_size, dtype=jnp.int32)
    normed, root_mean = normalize(states[0], gain)
    width = head.shape[1]
    features = normed.shape[1]
    digits = digit_count(width * vocab_size)
    place = RADIX ** jnp.arange(digits, dtype=jnp.int32)
    coded = ((target_ids[0][:, None] // place[None, :]) % RADIX).astype(jnp.bfloat16)
    coded = jnp.pad(coded, ((0, 0), (0, LANES - digits)))
    packed = lax.all_gather(jnp.concatenate([normed, coded], axis=1), "vocab", axis=0, tiled=True)
    group_normed = packed[:, :features]
    group_ids = jnp.sum(packed[:, features : features + digits].astype(jnp.int32) * place[None, :], axis=1)
    offset = vocab_index * width
    local_max, sums, expected, target = partial_stats(group_normed, head, group_ids, offset)
    rows = vocab_size * count
    home = own_order[vocab_index]
    root_rows = jnp.where(block_ids[:, None] == home, root_mean[None, :], 0.0)
    terms = jnp.stack([local_max, sums, expected, target]).reshape(4, vocab_size, count)
    source_of = jnp.sum(
        jnp.where(own_order[None, :] == block_ids[:, None], block_ids[None, :], 0), axis=1
    )
    routed = jnp.take(terms, source_of, axis=1)
    payload = jnp.concatenate([routed, root_rows[None]], axis=0).transpose(1, 0, 2)
    received = lax.all_to_all(payload, "vocab", 0, 0, tiled=True)
    shard_max, shard_sums, shard_expected, shard_target, shard_root = (
        received[:, 0], received[:, 1], received[:, 2], received[:, 3], received[:, 4]
    )
    peak = jnp.max(shard_max, axis=0)
    scale = jnp.exp(shard_max - peak[None, :])
    totals = jnp.sum(shard_sums * scale, axis=0)
    own_expected = jnp.sum(shard_expected * scale, axis=0)
    own_target = jnp.sum(shard_target, axis=0)
    own_root = jnp.sum(shard_root, axis=0)
    source_block = source_of[vocab_index]
    length_own = jnp.sum(jnp.where(block_ids == source_block, lengths[0], 0))
    keep = (jnp.arange(count, dtype=jnp.int32) < length_own).astype(jnp.float32)
    log_total = jnp.log(totals)
    log_prob = (own_target - peak - log_total) * keep
    entropy = (peak + log_total - own_expected / totals) * keep
    return (log_prob[None], entropy[None], (own_root * keep)[None], (peak * keep)[None])


def solution(mesh):
    in_specs = (
        P("grp", "vocab", None),
        P("grp", "vocab"),
        P("grp", None),
        P(),
        P(),
        P(None, "vocab"),
    )
    out_specs = (P("grp", "vocab"), P("grp", "vocab"), P("grp", "vocab"), P("grp", "vocab"))
    return jax.shard_map(shards, mesh=mesh, in_specs=in_specs, out_specs=out_specs, check_vma=False)
```

```python
import jax
import jax.numpy as jnp
from jax import lax
from jax.sharding import PartitionSpec as P

EPSILON = 1e-05
RADIX = 256
LANES = 128
RING_LIMIT = 8


def digit_count(total):
    digits = 1
    while RADIX**digits < total:
        digits += 1
    return digits


def normalize(block_states, gain):
    values = block_states.astype(jnp.float32)
    mean_square = jnp.mean(values * values, axis=-1)
    normed = (values * lax.rsqrt(mean_square + EPSILON)[:, None] * gain).astype(jnp.bfloat16)
    return (normed, jnp.sqrt(mean_square))


def ring_gather(block, size):
    pieces = [block]
    for shift in range(1, size):
        pieces.append(lax.ppermute(block, "vocab", [(i, (i + shift) % size) for i in range(size)]))
    return jnp.concatenate(pieces, axis=0)


def partial_stats(partial_logits, normed, columns, token_ids, offset):
    logits = partial_logits + jnp.dot(normed, columns, preferred_element_type=jnp.float32)
    local_max = jnp.max(logits, axis=1)
    weights = jnp.exp(logits - local_max[:, None])
    width = columns.shape[1]
    within = token_ids - offset
    inside = (within >= 0) & (within < width)
    picked = jnp.take_along_axis(logits, jnp.clip(within, 0, width - 1)[:, None], axis=1)[:, 0]
    return (
        local_max,
        jnp.sum(weights, axis=1),
        jnp.sum(weights * logits, axis=1),
        jnp.where(inside, picked, 0.0),
    )


def shards(states, target_ids, lengths, order, gain, head):
    count = states.shape[1]
    vocab_size = lax.axis_size("vocab")
    vocab_index = lax.axis_index("vocab")
    group_index = lax.axis_index("grp")
    own_order = lax.dynamic_index_in_dim(order, group_index, 0, keepdims=False)
    block_ids = jnp.arange(vocab_size, dtype=jnp.int32)
    normed, root_mean = normalize(states[0], gain)
    width = head.shape[1]
    features = normed.shape[1]
    digits = digit_count(width * vocab_size)
    place = RADIX ** jnp.arange(digits, dtype=jnp.int32)
    coded = ((target_ids[0][:, None] // place[None, :]) % RADIX).astype(jnp.bfloat16)
    coded = jnp.pad(coded, ((0, 0), (0, LANES - digits)))
    half = features // 2
    first = jnp.concatenate([normed[:, :half], coded], axis=1)
    second = normed[:, half:]
    if vocab_size <= RING_LIMIT:
        gathered_first = ring_gather(first, vocab_size)
        gathered_second = ring_gather(second, vocab_size)
        arrival = (vocab_index - block_ids) % vocab_size
    else:
        gathered_first = lax.all_gather(first, "vocab", axis=0, tiled=True)
        gathered_second = lax.all_gather(second, "vocab", axis=0, tiled=True)
        arrival = block_ids
    group_ids = jnp.sum(
        gathered_first[:, half : half + digits].astype(jnp.int32) * place[None, :], axis=1
    )
    offset = vocab_index * width
    partial_logits = jnp.dot(
        gathered_first[:, :half], head[:half], preferred_element_type=jnp.float32
    )
    local_max, sums, expected, target = partial_stats(
        partial_logits, gathered_second, head[half:], group_ids, offset
    )
    rows = vocab_size * count
    home = own_order[vocab_index]
    root_rows = jnp.where(block_ids[:, None] == home, root_mean[None, :], 0.0)
    terms = jnp.stack([local_max, sums, expected, target]).reshape(4, vocab_size, count)
    source_of = jnp.sum(
        jnp.where(own_order[None, :] == block_ids[:, None], block_ids[None, :], 0), axis=1
    )
    routed = jnp.take(terms, arrival[source_of], axis=1)
    payload = jnp.concatenate([routed, root_rows[None]], axis=0).transpose(1, 0, 2)
    received = lax.all_to_all(payload, "vocab", 0, 0, tiled=True)
    shard_max, shard_sums, shard_expected, shard_target, shard_root = (
        received[:, 0], received[:, 1], received[:, 2], received[:, 3], received[:, 4]
    )
    peak = jnp.max(shard_max, axis=0)
    scale = jnp.exp(shard_max - peak[None, :])
    totals = jnp.sum(shard_sums * scale, axis=0)
    own_expected = jnp.sum(shard_expected * scale, axis=0)
    own_target = jnp.sum(shard_target, axis=0)
    own_root = jnp.sum(shard_root, axis=0)
    source_block = source_of[vocab_index]
    length_own = jnp.sum(jnp.where(block_ids == source_block, lengths[0], 0))
    keep = (jnp.arange(count, dtype=jnp.int32) < length_own).astype(jnp.float32)
    log_total = jnp.log(totals)
    log_prob = (own_target - peak - log_total) * keep
    entropy = (peak + log_total - own_expected / totals) * keep
    return (log_prob[None], entropy[None], (own_root * keep)[None], (peak * keep)[None])


def solution(mesh):
    in_specs = (
        P("grp", "vocab", None),
        P("grp", "vocab"),
        P("grp", None),
        P(),
        P(),
        P(None, "vocab"),
    )
    out_specs = (P("grp", "vocab"), P("grp", "vocab"), P("grp", "vocab"), P("grp", "vocab"))
    return jax.shard_map(shards, mesh=mesh, in_specs=in_specs, out_specs=out_specs, check_vma=False)
```

```python
import jax
import jax.numpy as jnp
from jax import lax
from jax.sharding import PartitionSpec as P

EPSILON = 1e-05
RADIX = 256
LANES = 128


def digit_count(total):
    digits = 1
    while RADIX**digits < total:
        digits += 1
    return digits


def normalize(block_states, gain):
    values = block_states.astype(jnp.float32)
    mean_square = jnp.mean(values * values, axis=-1)
    normed = (values * lax.rsqrt(mean_square + EPSILON)[:, None] * gain).astype(jnp.bfloat16)
    return (normed, jnp.sqrt(mean_square))


def partial_stats(normed, columns, token_ids, offset):
    logits = jnp.dot(normed, columns, preferred_element_type=jnp.float32)
    local_max = jnp.max(logits, axis=1)
    weights = jnp.exp(logits - local_max[:, None])
    width = columns.shape[1]
    within = token_ids - offset
    inside = (within >= 0) & (within < width)
    picked = jnp.take_along_axis(logits, jnp.clip(within, 0, width - 1)[:, None], axis=1)[:, 0]
    return (
        local_max,
        jnp.sum(weights, axis=1),
        jnp.sum(weights * logits, axis=1),
        jnp.where(inside, picked, 0.0),
    )


def shards(states, target_ids, lengths, order, gain, head):
    count = states.shape[1]
    vocab_size = lax.axis_size("vocab")
    group_size = lax.axis_size("grp")
    vocab_index = lax.axis_index("vocab")
    group_index = lax.axis_index("grp")
    core = group_index % 2
    pair_base = group_index - core
    own_order = lax.dynamic_index_in_dim(order, group_index, 0, keepdims=False)
    block_ids = jnp.arange(vocab_size, dtype=jnp.int32)
    normed, root_mean = normalize(states[0], gain)
    width = head.shape[1]
    features = normed.shape[1]
    digits = digit_count(width * vocab_size)
    place = RADIX ** jnp.arange(digits, dtype=jnp.int32)
    coded = ((target_ids[0][:, None] // place[None, :]) % RADIX).astype(jnp.bfloat16)
    coded = jnp.pad(coded, ((0, 0), (0, LANES - digits)))
    packed = lax.all_gather(jnp.concatenate([normed, coded], axis=1), "vocab", axis=0, tiled=True)
    partner = lax.ppermute(
        packed, "grp", [(g, g ^ 1) for g in range(group_size)]
    )
    pair_rows = jnp.where(core == 0, jnp.concatenate([packed, partner]), jnp.concatenate([partner, packed]))
    pair_normed = pair_rows[:, :features]
    pair_ids = jnp.sum(pair_rows[:, features : features + digits].astype(jnp.int32) * place[None, :], axis=1)
    span = width // 2
    columns = lax.dynamic_slice_in_dim(head, core * span, span, 1)
    offset = vocab_index * width + core * span
    local_max, sums, expected, target = partial_stats(pair_normed, columns, pair_ids, offset)
    terms = jnp.stack([local_max, sums, expected, target]).reshape(4, 2, vocab_size, count)
    pair_order = lax.dynamic_slice_in_dim(order, pair_base, 2, 0)
    route = (pair_order[:, None, :] == block_ids[None, :, None]).astype(jnp.float32)
    routed = jnp.einsum("cjs,kcsr->jckr", route, terms, precision=lax.Precision.HIGHEST)
    group_ids = jnp.arange(group_size, dtype=jnp.int32)
    same_pair = (group_ids // 2 == pair_base // 2)[None, :, None, None]
    routed = jnp.take(routed, group_ids % 2, axis=1)
    stat_ids = jnp.arange(4, dtype=jnp.int32)[None, None, :, None]
    fill = jnp.where(stat_ids == 0, jnp.finfo(jnp.float32).min, 0.0)
    routed = jnp.where(same_pair, routed, fill)
    home = own_order[vocab_index]
    root_slot = (block_ids[:, None] == home) & (group_ids[None, :] == group_index)
    root_rows = jnp.where(root_slot[:, :, None], root_mean[None, None, :], 0.0)
    payload = jnp.concatenate([routed, root_rows[:, :, None, :]], axis=2)
    payload = payload.reshape(vocab_size * group_size, 5, count)
    received = lax.all_to_all(payload, ("vocab", "grp"), 0, 0, tiled=True)
    shard_max, shard_sums, shard_expected, shard_target, shard_root = (
        received[:, 0], received[:, 1], received[:, 2], received[:, 3], received[:, 4]
    )
    peak = jnp.max(shard_max, axis=0)
    scale = jnp.exp(shard_max - peak[None, :])
    totals = jnp.sum(shard_sums * scale, axis=0)
    own_expected = jnp.sum(shard_expected * scale, axis=0)
    own_target = jnp.sum(shard_target, axis=0)
    own_root = jnp.sum(shard_root, axis=0)
    source_block = jnp.sum(jnp.where(own_order == vocab_index, block_ids, 0))
    length_own = jnp.sum(jnp.where(block_ids == source_block, lengths[0], 0))
    keep = (jnp.arange(count, dtype=jnp.int32) < length_own).astype(jnp.float32)
    log_total = jnp.log(totals)
    log_prob = (own_target - peak - log_total) * keep
    entropy = (peak + log_total - own_expected / totals) * keep
    return (log_prob[None], entropy[None], (own_root * keep)[None], (peak * keep)[None])


def solution(mesh):
    in_specs = (
        P("grp", "vocab", None),
        P("grp", "vocab"),
        P("grp", None),
        P(),
        P(),
        P(None, "vocab"),
    )
    out_specs = (P("grp", "vocab"), P("grp", "vocab"), P("grp", "vocab"), P("grp", "vocab"))
    return jax.shard_map(shards, mesh=mesh, in_specs=in_specs, out_specs=out_specs, check_vma=False)
```

```python
import jax
import jax.numpy as jnp
from jax import lax
from jax.sharding import Mesh, PartitionSpec as P

EPSILON = 1e-05
RADIX = 256
VOCAB = ("vocab_hi", "vocab_lo")
LANES = 128


def digit_count(total):
    digits = 1
    while RADIX**digits < total:
        digits += 1
    return digits


def normalize(block_states, gain):
    values = block_states.astype(jnp.float32)
    mean_square = jnp.mean(values * values, axis=-1)
    normed = (values * lax.rsqrt(mean_square + EPSILON)[:, None] * gain).astype(jnp.bfloat16)
    return (normed, jnp.sqrt(mean_square))


def partial_stats(normed, columns, token_ids, offset):
    logits = jnp.dot(normed, columns, preferred_element_type=jnp.float32)
    local_max = jnp.max(logits, axis=1)
    weights = jnp.exp(logits - local_max[:, None])
    width = columns.shape[1]
    within = token_ids - offset
    inside = (within >= 0) & (within < width)
    picked = jnp.take_along_axis(logits, jnp.clip(within, 0, width - 1)[:, None], axis=1)[:, 0]
    return (
        local_max,
        jnp.sum(weights, axis=1),
        jnp.sum(weights * logits, axis=1),
        jnp.where(inside, picked, 0.0),
    )


def shards(states, target_ids, lengths, order, gain, head):
    count = states.shape[1]
    vocab_size = lax.axis_size(VOCAB)
    group_size = lax.axis_size("grp")
    vocab_index = lax.axis_index(VOCAB)
    group_index = lax.axis_index("grp")
    core = group_index % 2
    pair_base = group_index - core
    own_order = lax.dynamic_index_in_dim(order, group_index, 0, keepdims=False)
    block_ids = jnp.arange(vocab_size, dtype=jnp.int32)
    normed, root_mean = normalize(states[0], gain)
    width = head.shape[1]
    features = normed.shape[1]
    digits = digit_count(width * vocab_size)
    place = RADIX ** jnp.arange(digits, dtype=jnp.int32)
    coded = ((target_ids[0][:, None] // place[None, :]) % RADIX).astype(jnp.bfloat16)
    coded = jnp.pad(coded, ((0, 0), (0, LANES - digits)))
    packed = jnp.concatenate([normed, coded], axis=1)
    packed = lax.all_gather(packed, "vocab_lo", axis=0, tiled=True)
    packed = lax.all_gather(packed, "vocab_hi", axis=0, tiled=True)
    partner = lax.ppermute(
        packed, "grp", [(g, g ^ 1) for g in range(group_size)]
    )
    pair_rows = jnp.where(core == 0, jnp.concatenate([packed, partner]), jnp.concatenate([partner, packed]))
    pair_normed = pair_rows[:, :features]
    pair_ids = jnp.sum(pair_rows[:, features : features + digits].astype(jnp.int32) * place[None, :], axis=1)
    span = width // 2
    columns = lax.dynamic_slice_in_dim(head, core * span, span, 1)
    offset = vocab_index * width + core * span
    local_max, sums, expected, target = partial_stats(pair_normed, columns, pair_ids, offset)
    terms = jnp.stack([local_max, sums, expected, target]).reshape(4, 2, vocab_size, count)
    pair_order = lax.dynamic_slice_in_dim(order, pair_base, 2, 0)
    route = (pair_order[:, None, :] == block_ids[None, :, None]).astype(jnp.float32)
    routed = jnp.einsum("cjs,kcsr->jckr", route, terms, precision=lax.Precision.HIGHEST)
    group_ids = jnp.arange(group_size, dtype=jnp.int32)
    same_pair = (group_ids // 2 == pair_base // 2)[None, :, None, None]
    routed = jnp.take(routed, group_ids % 2, axis=1)
    stat_ids = jnp.arange(4, dtype=jnp.int32)[None, None, :, None]
    fill = jnp.where(stat_ids == 0, jnp.finfo(jnp.float32).min, 0.0)
    routed = jnp.where(same_pair, routed, fill)
    home = own_order[vocab_index]
    root_slot = (block_ids[:, None] == home) & (group_ids[None, :] == group_index)
    root_rows = jnp.where(root_slot[:, :, None], root_mean[None, None, :], 0.0)
    payload = jnp.concatenate([routed, root_rows[:, :, None, :]], axis=2)
    payload = payload.reshape(vocab_size * group_size, 5, count)
    received = lax.all_to_all(payload, VOCAB + ("grp",), 0, 0, tiled=True)
    shard_max, shard_sums, shard_expected, shard_target, shard_root = (
        received[:, 0], received[:, 1], received[:, 2], received[:, 3], received[:, 4]
    )
    peak = jnp.max(shard_max, axis=0)
    scale = jnp.exp(shard_max - peak[None, :])
    totals = jnp.sum(shard_sums * scale, axis=0)
    own_expected = jnp.sum(shard_expected * scale, axis=0)
    own_target = jnp.sum(shard_target, axis=0)
    own_root = jnp.sum(shard_root, axis=0)
    source_block = jnp.sum(jnp.where(own_order == vocab_index, block_ids, 0))
    length_own = jnp.sum(jnp.where(block_ids == source_block, lengths[0], 0))
    keep = (jnp.arange(count, dtype=jnp.int32) < length_own).astype(jnp.float32)
    log_total = jnp.log(totals)
    log_prob = (own_target - peak - log_total) * keep
    entropy = (peak + log_total - own_expected / totals) * keep
    return (log_prob[None], entropy[None], (own_root * keep)[None], (peak * keep)[None])


def solution(mesh):
    vocab_size, group_size = mesh.devices.shape
    low = 2 if vocab_size % 2 == 0 else 1
    split = Mesh(mesh.devices.reshape(vocab_size // low, low, group_size), VOCAB + ("grp",))
    in_specs = (
        P("grp", VOCAB, None),
        P("grp", VOCAB),
        P("grp", None),
        P(),
        P(),
        P(None, VOCAB),
    )
    out_specs = (P("grp", VOCAB),) * 4
    return jax.shard_map(shards, mesh=split, in_specs=in_specs, out_specs=out_specs, check_vma=False)
```

```python
from functools import partial

import jax
import jax.numpy as jnp
from jax import lax
from jax.experimental import pallas as pl
from jax.experimental.pallas import tpu as pltpu
from jax.sharding import Mesh, PartitionSpec as P

EPSILON = 1e-05
RADIX = 256
VOCAB = ("vocab_hi", "vocab_lo")
LANES = 128
TILE = 512
ROW_TILE = 256


def digit_count(total):
    digits = 1
    while RADIX**digits < total:
        digits += 1
    return digits


def normalize(block_states, gain):
    values = block_states.astype(jnp.float32)
    mean_square = jnp.mean(values * values, axis=-1)
    normed = (values * lax.rsqrt(mean_square + EPSILON)[:, None] * gain).astype(jnp.bfloat16)
    return (normed, jnp.sqrt(mean_square))


def partial_stats(normed, columns, token_ids, offset):
    logits = jnp.dot(normed, columns, preferred_element_type=jnp.float32)
    local_max = jnp.max(logits, axis=1)
    weights = jnp.exp(logits - local_max[:, None])
    width = columns.shape[1]
    within = token_ids - offset
    inside = (within >= 0) & (within < width)
    picked = jnp.take_along_axis(logits, jnp.clip(within, 0, width - 1)[:, None], axis=1)[:, 0]
    return (
        local_max,
        jnp.sum(weights, axis=1),
        jnp.sum(weights * logits, axis=1),
        jnp.where(inside, picked, 0.0),
    )


def stats_kernel(scalars, rows_ref, codes_ref, head_ref, max_ref, sum_ref, exp_ref, tgt_ref, *, tile, digits):
    step = pl.program_id(1)

    @pl.when(step == 0)
    def _():
        max_ref[...] = jnp.full(max_ref.shape, -jnp.inf, jnp.float32)
        sum_ref[...] = jnp.zeros(sum_ref.shape, jnp.float32)
        exp_ref[...] = jnp.zeros(exp_ref.shape, jnp.float32)
        tgt_ref[...] = jnp.zeros(tgt_ref.shape, jnp.float32)

    logits = jnp.dot(rows_ref[...], head_ref[...], preferred_element_type=jnp.float32)
    old_max = max_ref[...]
    new_max = jnp.maximum(old_max, jnp.max(logits, axis=1, keepdims=True))
    rescale = jnp.exp(old_max - new_max)
    weights = jnp.exp(logits - new_max)
    sum_ref[...] = sum_ref[...] * rescale + jnp.sum(weights, axis=1, keepdims=True)
    exp_ref[...] = exp_ref[...] * rescale + jnp.sum(weights * logits, axis=1, keepdims=True)
    max_ref[...] = new_max
    codes = codes_ref[...].astype(jnp.float32)
    lane = lax.broadcasted_iota(jnp.int32, codes.shape, 1)
    place = jnp.zeros(codes.shape, jnp.float32)
    for k in range(digits):
        place = jnp.where(lane == k, float(RADIX**k), place)
    token = jnp.sum(codes * place, axis=1, keepdims=True)
    column = scalars[1] + step * tile + lax.broadcasted_iota(jnp.int32, logits.shape, 1)
    hit = column.astype(jnp.float32) == token
    tgt_ref[...] += jnp.sum(jnp.where(hit, logits, 0.0), axis=1, keepdims=True)


def fused_stats(packed, head, first_block, first_column, features, span, digits):
    rows = packed.shape[0]
    tile = min(TILE, span)
    row_tile = rows
    while row_tile > ROW_TILE and row_tile % 2 == 0:
        row_tile //= 2
    grid = (rows // row_tile, span // tile)
    scalars = jnp.stack([first_block, first_column]).astype(jnp.int32)
    stat = jax.ShapeDtypeStruct((rows, 1), jnp.float32)
    stat_spec = pl.BlockSpec((row_tile, 1), lambda i, j, s: (i, 0))
    return pl.pallas_call(
        partial(stats_kernel, tile=tile, digits=digits),
        out_shape=(stat,) * 4,
        grid_spec=pltpu.PrefetchScalarGridSpec(
            num_scalar_prefetch=1,
            grid=grid,
            in_specs=[
                pl.BlockSpec((row_tile, features), lambda i, j, s: (i, 0)),
                pl.BlockSpec((row_tile, LANES), lambda i, j, s: (i, features // LANES)),
                pl.BlockSpec((features, tile), lambda i, j, s: (0, s[0] + j)),
            ],
            out_specs=[stat_spec] * 4,
        ),
        compiler_params=pltpu.CompilerParams(dimension_semantics=("arbitrary", "arbitrary")),
    )(scalars, packed, packed, head)


def shards(states, target_ids, lengths, order, gain, head):
    count = states.shape[1]
    vocab_size = lax.axis_size(VOCAB)
    group_size = lax.axis_size("grp")
    vocab_index = lax.axis_index(VOCAB)
    group_index = lax.axis_index("grp")
    core = group_index % 2
    pair_base = group_index - core
    own_order = lax.dynamic_index_in_dim(order, group_index, 0, keepdims=False)
    block_ids = jnp.arange(vocab_size, dtype=jnp.int32)
    normed, root_mean = normalize(states[0], gain)
    width = head.shape[1]
    features = normed.shape[1]
    digits = digit_count(width * vocab_size)
    place = RADIX ** jnp.arange(digits, dtype=jnp.int32)
    coded = ((target_ids[0][:, None] // place[None, :]) % RADIX).astype(jnp.bfloat16)
    coded = jnp.pad(coded, ((0, 0), (0, LANES - digits)))
    packed = jnp.concatenate([normed, coded], axis=1)
    packed = lax.all_gather(packed, "vocab_lo", axis=0, tiled=True)
    packed = lax.all_gather(packed, "vocab_hi", axis=0, tiled=True)
    partner = lax.ppermute(
        packed, "grp", [(g, g ^ 1) for g in range(group_size)]
    )
    pair_rows = jnp.where(core == 0, jnp.concatenate([packed, partner]), jnp.concatenate([partner, packed]))
    span = width // 2
    first_column = vocab_index * width + core * span
    local_max, sums, expected, target = (
        stat[:, 0]
        for stat in fused_stats(
            pair_rows, head, core * (span // min(TILE, span)), first_column, features, span, digits
        )
    )
    terms = jnp.stack([local_max, sums, expected, target]).reshape(4, 2, vocab_size, count)
    pair_order = lax.dynamic_slice_in_dim(order, pair_base, 2, 0)
    route = (pair_order[:, None, :] == block_ids[None, :, None]).astype(jnp.float32)
    routed = jnp.einsum("cjs,kcsr->jckr", route, terms, precision=lax.Precision.HIGHEST)
    group_ids = jnp.arange(group_size, dtype=jnp.int32)
    same_pair = (group_ids // 2 == pair_base // 2)[None, :, None, None]
    routed = jnp.take(routed, group_ids % 2, axis=1)
    stat_ids = jnp.arange(4, dtype=jnp.int32)[None, None, :, None]
    fill = jnp.where(stat_ids == 0, jnp.finfo(jnp.float32).min, 0.0)
    routed = jnp.where(same_pair, routed, fill)
    home = own_order[vocab_index]
    root_slot = (block_ids[:, None] == home) & (group_ids[None, :] == group_index)
    root_rows = jnp.where(root_slot[:, :, None], root_mean[None, None, :], 0.0)
    payload = jnp.concatenate([routed, root_rows[:, :, None, :]], axis=2)
    payload = payload.reshape(vocab_size * group_size, 5, count)
    received = lax.all_to_all(payload, VOCAB + ("grp",), 0, 0, tiled=True)
    shard_max, shard_sums, shard_expected, shard_target, shard_root = (
        received[:, 0], received[:, 1], received[:, 2], received[:, 3], received[:, 4]
    )
    peak = jnp.max(shard_max, axis=0)
    scale = jnp.exp(shard_max - peak[None, :])
    totals = jnp.sum(shard_sums * scale, axis=0)
    own_expected = jnp.sum(shard_expected * scale, axis=0)
    own_target = jnp.sum(shard_target, axis=0)
    own_root = jnp.sum(shard_root, axis=0)
    source_block = jnp.sum(jnp.where(own_order == vocab_index, block_ids, 0))
    length_own = jnp.sum(jnp.where(block_ids == source_block, lengths[0], 0))
    keep = (jnp.arange(count, dtype=jnp.int32) < length_own).astype(jnp.float32)
    log_total = jnp.log(totals)
    log_prob = (own_target - peak - log_total) * keep
    entropy = (peak + log_total - own_expected / totals) * keep
    return (log_prob[None], entropy[None], (own_root * keep)[None], (peak * keep)[None])


def solution(mesh):
    vocab_size, group_size = mesh.devices.shape
    low = 2 if vocab_size % 2 == 0 else 1
    split = Mesh(mesh.devices.reshape(vocab_size // low, low, group_size), VOCAB + ("grp",))
    in_specs = (
        P("grp", VOCAB, None),
        P("grp", VOCAB),
        P("grp", None),
        P(),
        P(),
        P(None, VOCAB),
    )
    out_specs = (P("grp", VOCAB),) * 4
    return jax.shard_map(shards, mesh=split, in_specs=in_specs, out_specs=out_specs, check_vma=False)
```

```python
import jax
import jax.numpy as jnp
from jax import lax
from jax.sharding import Mesh, PartitionSpec as P

EPSILON = 1e-05
RADIX_BITS = 8
RADIX = 1 << RADIX_BITS
VOCAB = ("vocab_hi", "vocab_lo")
GROUP = ("grp_hi", "grp_lo")
LANES = 128


def digit_count(total):
    digits = 1
    while RADIX**digits < total:
        digits += 1
    return digits


def normalize(block_states, gain):
    values = block_states.astype(jnp.float32)
    mean_square = jnp.mean(values * values, axis=-1)
    normed = (values * lax.rsqrt(mean_square + EPSILON)[:, None] * gain).astype(jnp.bfloat16)
    return (normed, jnp.sqrt(mean_square))


def partial_stats(normed, columns, token_ids, offset):
    logits = jnp.dot(normed, columns, preferred_element_type=jnp.float32)
    local_max = jnp.max(logits, axis=1)
    weights = jnp.exp(logits - local_max[:, None])
    within = token_ids - offset
    column = lax.broadcasted_iota(jnp.int32, logits.shape, 1)
    return (
        local_max,
        jnp.sum(weights, axis=1),
        jnp.sum(weights * logits, axis=1),
        jnp.sum(jnp.where(column == within[:, None], logits, 0.0), axis=1),
    )


def shards(states, target_ids, lengths, order, gain, head):
    count = states.shape[1]
    vocab_size = lax.axis_size(VOCAB)
    group_size = lax.axis_size(GROUP)
    vocab_index = lax.axis_index(VOCAB)
    group_index = lax.axis_index(GROUP)
    core = group_index % 2
    pair_base = group_index - core
    own_order = lax.dynamic_index_in_dim(order, group_index, 0, keepdims=False)
    block_ids = jnp.arange(vocab_size, dtype=jnp.int32)
    normed, root_mean = normalize(states[0], gain)
    width = head.shape[1]
    features = normed.shape[1]
    digits = digit_count(width * vocab_size)
    place = RADIX ** jnp.arange(digits, dtype=jnp.int32)
    shifts = RADIX_BITS * jnp.arange(digits, dtype=jnp.int32)
    coded = ((target_ids[0][:, None] >> shifts[None, :]) & (RADIX - 1)).astype(jnp.bfloat16)
    coded = jnp.pad(coded, ((0, 0), (0, LANES - digits)))
    packed = jnp.concatenate([normed, coded], axis=1)
    packed = lax.all_gather(packed, "vocab_lo", axis=0, tiled=True)
    packed = lax.all_gather(packed, "vocab_hi", axis=0, tiled=True)
    partner = lax.ppermute(packed, "grp_lo", [(0, 1), (1, 0)])
    pair_rows = jnp.where(core == 0, jnp.concatenate([packed, partner]), jnp.concatenate([partner, packed]))
    pair_normed = pair_rows[:, :features]
    pair_ids = jnp.sum(pair_rows[:, features : features + digits].astype(jnp.int32) * place[None, :], axis=1)
    span = width // 2
    columns = lax.dynamic_slice_in_dim(head, core * span, span, 1)
    offset = vocab_index * width + core * span
    local_max, sums, expected, target = partial_stats(pair_normed, columns, pair_ids, offset)
    terms = jnp.stack([local_max, sums, expected, target]).reshape(4, 2, vocab_size, count)
    pair_order = lax.dynamic_slice_in_dim(order, pair_base, 2, 0)
    route = (pair_order[:, None, :] == block_ids[None, :, None]).astype(jnp.float32)
    routed = jnp.einsum("cjs,kcsr->jckr", route, terms, precision=lax.Precision.HIGHEST)
    group_ids = jnp.arange(2, dtype=jnp.int32)
    home = own_order[vocab_index]
    root_slot = (block_ids[:, None] == home) & (group_ids[None, :] == core)
    root_rows = jnp.where(root_slot[:, :, None], root_mean[None, None, :], 0.0)
    payload = jnp.concatenate([routed, root_rows[:, :, None, :]], axis=2)
    payload = payload.reshape(vocab_size * 2, 5, count)
    received = lax.all_to_all(payload, VOCAB + ("grp_lo",), 0, 0, tiled=True)
    shard_max, shard_sums, shard_expected, shard_target, shard_root = (
        received[:, 0], received[:, 1], received[:, 2], received[:, 3], received[:, 4]
    )
    peak = jnp.max(shard_max, axis=0)
    scale = jnp.exp(shard_max - peak[None, :])
    totals = jnp.sum(shard_sums * scale, axis=0)
    own_expected = jnp.sum(shard_expected * scale, axis=0)
    own_target = jnp.sum(shard_target, axis=0)
    own_root = jnp.sum(shard_root, axis=0)
    source_block = jnp.sum(jnp.where(own_order == vocab_index, block_ids, 0))
    length_own = jnp.sum(jnp.where(block_ids == source_block, lengths[0], 0))
    keep = (jnp.arange(count, dtype=jnp.int32) < length_own).astype(jnp.float32)
    log_total = jnp.log(totals)
    log_prob = (own_target - peak - log_total) * keep
    entropy = (peak + log_total - own_expected / totals) * keep
    return (log_prob[None], entropy[None], (own_root * keep)[None], (peak * keep)[None])


def solution(mesh):
    vocab_size, group_size = mesh.devices.shape
    assert vocab_size % 2 == 0 and group_size % 2 == 0
    split = Mesh(mesh.devices.reshape(vocab_size // 2, 2, group_size // 2, 2), VOCAB + GROUP)
    in_specs = (
        P(GROUP, VOCAB, None),
        P(GROUP, VOCAB),
        P(GROUP, None),
        P(),
        P(),
        P(None, VOCAB),
    )
    out_specs = (P(GROUP, VOCAB),) * 4
    return jax.shard_map(shards, mesh=split, in_specs=in_specs, out_specs=out_specs, check_vma=False)
```

```python
from functools import partial

import jax
import jax.numpy as jnp
from jax import lax
from jax.experimental import pallas as pl
from jax.sharding import Mesh, PartitionSpec as P

EPSILON = 1e-05
RADIX_BITS = 8
RADIX = 1 << RADIX_BITS
VOCAB = ("vocab_hi", "vocab_lo")
GROUP = ("grp_hi", "grp_lo")
LANES = 128


def digit_count(total):
    digits = 1
    while RADIX**digits < total:
        digits += 1
    return digits


def normalize(block_states, gain):
    values = block_states.astype(jnp.float32)
    mean_square = jnp.mean(values * values, axis=-1)
    normed = (values * lax.rsqrt(mean_square + EPSILON)[:, None] * gain).astype(jnp.bfloat16)
    return (normed, jnp.sqrt(mean_square))


def partial_stats(normed, columns, token_ids, offset):
    logits = jnp.dot(normed, columns, preferred_element_type=jnp.float32)
    local_max = jnp.max(logits, axis=1)
    weights = jnp.exp(logits - local_max[:, None])
    within = token_ids - offset
    column = lax.broadcasted_iota(jnp.int32, logits.shape, 1)
    return (
        local_max,
        jnp.sum(weights, axis=1),
        jnp.sum(weights * logits, axis=1),
        jnp.sum(jnp.where(column == within[:, None], logits, 0.0), axis=1),
    )


def pack_kernel(states_ref, gain_ref, ids_ref, out_ref, *, features, digits):
    values = states_ref[...].astype(jnp.float32)
    mean_square = jnp.mean(values * values, axis=1, keepdims=True)
    normed = (values * lax.rsqrt(mean_square + EPSILON) * gain_ref[...]).astype(jnp.bfloat16)
    out_ref[:, :features] = normed
    ids = ids_ref[...]
    count = ids.shape[1]
    row = lax.broadcasted_iota(jnp.int32, (count, count), 0)
    col = lax.broadcasted_iota(jnp.int32, (count, count), 1)
    token = jnp.sum(jnp.where(row == col, jnp.broadcast_to(ids, (count, count)), 0), axis=1, keepdims=True)
    lane = lax.broadcasted_iota(jnp.int32, (count, LANES), 1)
    code = jnp.zeros((count, LANES), jnp.int32)
    for k in range(digits):
        code = jnp.where(lane == k, (token >> (RADIX_BITS * k)) & (RADIX - 1), code)
    out_ref[:, features:] = code.astype(jnp.float32).astype(jnp.bfloat16)


def pack_rows(block_states, gain, token_ids, digits):
    count, features = block_states.shape
    return pl.pallas_call(
        partial(pack_kernel, features=features, digits=digits),
        out_shape=jax.ShapeDtypeStruct((count, features + LANES), jnp.bfloat16),
    )(block_states, gain.reshape(1, features), token_ids)


def shards(states, target_ids, lengths, order, gain, head):
    count = states.shape[1]
    vocab_size = lax.axis_size(VOCAB)
    group_size = lax.axis_size(GROUP)
    vocab_index = lax.axis_index(VOCAB)
    group_index = lax.axis_index(GROUP)
    core = group_index % 2
    pair_base = group_index - core
    own_order = lax.dynamic_index_in_dim(order, group_index, 0, keepdims=False)
    block_ids = jnp.arange(vocab_size, dtype=jnp.int32)
    root_mean = jnp.sqrt(jnp.mean(jnp.square(states[0].astype(jnp.float32)), axis=-1))
    width = head.shape[1]
    features = states.shape[2]
    digits = digit_count(width * vocab_size)
    place = RADIX ** jnp.arange(digits, dtype=jnp.int32)
    packed = pack_rows(states[0], gain, target_ids, digits)
    packed = lax.all_gather(packed, "vocab_lo", axis=0, tiled=True)
    packed = lax.all_gather(packed, "vocab_hi", axis=0, tiled=True)
    partner = lax.ppermute(packed, "grp_lo", [(0, 1), (1, 0)])
    pair_rows = jnp.concatenate([packed, partner])
    pair_normed = pair_rows[:, :features]
    pair_ids = jnp.sum(pair_rows[:, features : features + digits].astype(jnp.int32) * place[None, :], axis=1)
    span = width // 2
    columns = lax.dynamic_slice_in_dim(head, core * span, span, 1)
    offset = vocab_index * width + core * span
    local_max, sums, expected, target = partial_stats(pair_normed, columns, pair_ids, offset)
    terms = jnp.stack([local_max, sums, expected, target]).reshape(4, 2, vocab_size, count)
    pair_order = lax.dynamic_slice_in_dim(order, pair_base, 2, 0)
    pair_order = jnp.where(core == 0, pair_order, pair_order[::-1])
    route = (pair_order[:, None, :] == block_ids[None, :, None]).astype(jnp.float32)
    routed = jnp.einsum("cjs,kcsr->jckr", route, terms, precision=lax.Precision.HIGHEST)
    routed = jnp.where(core == 0, routed, routed[:, ::-1])
    group_ids = jnp.arange(2, dtype=jnp.int32)
    home = own_order[vocab_index]
    root_slot = (block_ids[:, None] == home) & (group_ids[None, :] == core)
    root_rows = jnp.where(root_slot[:, :, None], root_mean[None, None, :], 0.0)
    payload = jnp.concatenate([routed, root_rows[:, :, None, :]], axis=2)
    payload = payload.reshape(vocab_size * 2, 5, count)
    received = lax.all_to_all(payload, VOCAB + ("grp_lo",), 0, 0, tiled=True)
    shard_max, shard_sums, shard_expected, shard_target, shard_root = (
        received[:, 0], received[:, 1], received[:, 2], received[:, 3], received[:, 4]
    )
    peak = jnp.max(shard_max, axis=0)
    scale = jnp.exp(shard_max - peak[None, :])
    totals = jnp.sum(shard_sums * scale, axis=0)
    own_expected = jnp.sum(shard_expected * scale, axis=0)
    own_target = jnp.sum(shard_target, axis=0)
    own_root = jnp.sum(shard_root, axis=0)
    source_block = jnp.sum(jnp.where(own_order == vocab_index, block_ids, 0))
    length_own = jnp.sum(jnp.where(block_ids == source_block, lengths[0], 0))
    keep = (jnp.arange(count, dtype=jnp.int32) < length_own).astype(jnp.float32)
    log_total = jnp.log(totals)
    log_prob = (own_target - peak - log_total) * keep
    entropy = (peak + log_total - own_expected / totals) * keep
    return (log_prob[None], entropy[None], (own_root * keep)[None], (peak * keep)[None])


def solution(mesh):
    vocab_size, group_size = mesh.devices.shape
    assert vocab_size % 2 == 0 and group_size % 2 == 0
    split = Mesh(mesh.devices.reshape(vocab_size // 2, 2, group_size // 2, 2), VOCAB + GROUP)
    in_specs = (
        P(GROUP, VOCAB, None),
        P(GROUP, VOCAB),
        P(GROUP, None),
        P(),
        P(),
        P(None, VOCAB),
    )
    out_specs = (P(GROUP, VOCAB),) * 4
    return jax.shard_map(shards, mesh=split, in_specs=in_specs, out_specs=out_specs, check_vma=False)
```

```python
from functools import partial

import jax
import jax.numpy as jnp
from jax import lax
from jax.experimental import pallas as pl
from jax.sharding import Mesh, PartitionSpec as P

EPSILON = 1e-05
RADIX_BITS = 8
RADIX = 1 << RADIX_BITS
VOCAB = ("vocab_hi", "vocab_lo")
GROUP = ("grp_hi", "grp_lo")
LANES = 128


def digit_count(total):
    digits = 1
    while RADIX**digits < total:
        digits += 1
    return digits


def normalize(block_states, gain):
    values = block_states.astype(jnp.float32)
    mean_square = jnp.mean(values * values, axis=-1)
    normed = (values * lax.rsqrt(mean_square + EPSILON)[:, None] * gain).astype(jnp.bfloat16)
    return (normed, jnp.sqrt(mean_square))


def partial_stats(normed, columns, token_ids, offset):
    logits = jnp.dot(normed, columns, preferred_element_type=jnp.float32)
    local_max = jnp.max(logits, axis=1)
    weights = jnp.exp(logits - local_max[:, None])
    within = token_ids - offset
    column = lax.broadcasted_iota(jnp.int32, logits.shape, 1)
    return (
        local_max,
        jnp.sum(weights, axis=1),
        jnp.sum(weights * logits, axis=1),
        jnp.sum(jnp.where(column == within[:, None], logits, 0.0), axis=1),
    )


def pack_kernel(states_ref, gain_ref, ids_ref, out_ref, *, features, digits):
    values = states_ref[...].astype(jnp.float32)
    mean_square = jnp.mean(values * values, axis=1, keepdims=True)
    normed = (values * lax.rsqrt(mean_square + EPSILON) * gain_ref[...]).astype(jnp.bfloat16)
    out_ref[:, :features] = normed
    ids = ids_ref[...]
    count = ids.shape[1]
    row = lax.broadcasted_iota(jnp.int32, (count, count), 0)
    col = lax.broadcasted_iota(jnp.int32, (count, count), 1)
    token = jnp.sum(jnp.where(row == col, jnp.broadcast_to(ids, (count, count)), 0), axis=1, keepdims=True)
    lane = lax.broadcasted_iota(jnp.int32, (count, LANES), 1)
    code = jnp.zeros((count, LANES), jnp.int32)
    for k in range(digits):
        code = jnp.where(lane == k, (token >> (RADIX_BITS * k)) & (RADIX - 1), code)
    out_ref[:, features:] = code.astype(jnp.float32).astype(jnp.bfloat16)


def pack_rows(block_states, gain, token_ids, digits):
    count, features = block_states.shape
    return pl.pallas_call(
        partial(pack_kernel, features=features, digits=digits),
        out_shape=jax.ShapeDtypeStruct((count, features + LANES), jnp.bfloat16),
    )(block_states, gain.reshape(1, features), token_ids)


def shards(states, target_ids, lengths, order, gain, head):
    count = states.shape[1]
    vocab_size = lax.axis_size(VOCAB)
    group_size = lax.axis_size(GROUP)
    vocab_index = lax.axis_index(VOCAB)
    group_index = lax.axis_index(GROUP)
    core = group_index % 2
    pair_base = group_index - core
    own_order = lax.dynamic_index_in_dim(order, group_index, 0, keepdims=False)
    block_ids = jnp.arange(vocab_size, dtype=jnp.int32)
    root_mean = jnp.sqrt(jnp.mean(jnp.square(states[0].astype(jnp.float32)), axis=-1))
    width = head.shape[1]
    features = states.shape[2]
    digits = digit_count(width * vocab_size)
    place = RADIX ** jnp.arange(digits, dtype=jnp.int32)
    packed = pack_rows(states[0], gain, target_ids, digits)
    packed = lax.all_gather(packed, "vocab_lo", axis=0, tiled=True)
    packed = lax.all_gather(packed, "vocab_hi", axis=0, tiled=True)
    partner = lax.ppermute(packed, "grp_lo", [(0, 1), (1, 0)])
    pair_rows = jnp.where(core == 0, jnp.concatenate([packed, partner]), jnp.concatenate([partner, packed]))
    pair_normed = pair_rows[:, :features]
    pair_ids = jnp.sum(pair_rows[:, features : features + digits].astype(jnp.int32) * place[None, :], axis=1)
    span = width // 2
    columns = lax.dynamic_slice_in_dim(head, core * span, span, 1)
    offset = vocab_index * width + core * span
    local_max, sums, expected, target = partial_stats(pair_normed, columns, pair_ids, offset)
    terms = jnp.stack([local_max, sums, expected, target]).reshape(4, 2, vocab_size, count)
    pair_order = lax.dynamic_slice_in_dim(order, pair_base, 2, 0)
    route = (pair_order[:, None, :] == block_ids[None, :, None]).astype(jnp.float32)
    routed = jnp.einsum("cjs,kcsr->jckr", route, terms, precision=lax.Precision.HIGHEST)
    group_ids = jnp.arange(2, dtype=jnp.int32)
    home = own_order[vocab_index]
    root_slot = (block_ids[:, None] == home) & (group_ids[None, :] == core)
    root_rows = jnp.where(root_slot[:, :, None], root_mean[None, None, :], 0.0)
    payload = jnp.concatenate([routed, root_rows[:, :, None, :]], axis=2)
    payload = payload.reshape(vocab_size * 2, 5, count)
    received = lax.all_to_all(payload, VOCAB + ("grp_lo",), 0, 0, tiled=True)
    shard_max, shard_sums, shard_expected, shard_target, shard_root = (
        received[:, 0], received[:, 1], received[:, 2], received[:, 3], received[:, 4]
    )
    peak = jnp.max(shard_max, axis=0)
    scale = jnp.exp(shard_max - peak[None, :])
    totals = jnp.sum(shard_sums * scale, axis=0)
    own_expected = jnp.sum(shard_expected * scale, axis=0)
    own_target = jnp.sum(shard_target, axis=0)
    own_root = jnp.sum(shard_root, axis=0)
    source_block = jnp.sum(jnp.where(own_order == vocab_index, block_ids, 0))
    length_own = jnp.sum(jnp.where(block_ids == source_block, lengths[0], 0))
    keep = (jnp.arange(count, dtype=jnp.int32) < length_own).astype(jnp.float32)
    log_total = jnp.log(totals)
    log_prob = (own_target - peak - log_total) * keep
    entropy = (peak + log_total - own_expected / totals) * keep
    return (log_prob[None], entropy[None], (own_root * keep)[None], (peak * keep)[None])


def solution(mesh):
    vocab_size, group_size = mesh.devices.shape
    assert vocab_size % 2 == 0 and group_size % 2 == 0
    split = Mesh(mesh.devices.reshape(vocab_size // 2, 2, group_size // 2, 2), VOCAB + GROUP)
    in_specs = (
        P(GROUP, VOCAB, None),
        P(GROUP, VOCAB),
        P(GROUP, None),
        P(),
        P(),
        P(None, VOCAB),
    )
    out_specs = (P(GROUP, VOCAB),) * 4
    return jax.shard_map(shards, mesh=split, in_specs=in_specs, out_specs=out_specs, check_vma=False)
```

```python
import jax
import jax.numpy as jnp
from jax import lax
from jax.sharding import Mesh, PartitionSpec as P

EPSILON = 1e-05
RADIX_BITS = 8
RADIX = 1 << RADIX_BITS
VOCAB = ("vocab_hi", "vocab_lo")
GROUP = ("grp_hi", "grp_lo")
LANES = 128
PIPELINE_LIMIT = 4


def digit_count(total):
    digits = 1
    while RADIX**digits < total:
        digits += 1
    return digits


def normalize(block_states, gain):
    values = block_states.astype(jnp.float32)
    mean_square = jnp.mean(values * values, axis=-1)
    normed = (values * lax.rsqrt(mean_square + EPSILON)[:, None] * gain).astype(jnp.bfloat16)
    return (normed, jnp.sqrt(mean_square))


def partial_stats(rows, columns, features, digits, place, offset):
    token_ids = jnp.sum(rows[:, features : features + digits].astype(jnp.int32) * place[None, :], axis=1)
    logits = jnp.dot(rows[:, :features], columns, preferred_element_type=jnp.float32)
    local_max = jnp.max(logits, axis=1)
    weights = jnp.exp(logits - local_max[:, None])
    within = token_ids - offset
    column = lax.broadcasted_iota(jnp.int32, logits.shape, 1)
    return (
        local_max,
        jnp.sum(weights, axis=1),
        jnp.sum(weights * logits, axis=1),
        jnp.sum(jnp.where(column == within[:, None], logits, 0.0), axis=1),
    )

def shards(states, target_ids, lengths, order, gain, head):
    count = states.shape[1]
    vocab_size = lax.axis_size(VOCAB)
    group_size = lax.axis_size(GROUP)
    vocab_index = lax.axis_index(VOCAB)
    group_index = lax.axis_index(GROUP)
    core = group_index % 2
    pair_base = group_index - core
    own_order = lax.dynamic_index_in_dim(order, group_index, 0, keepdims=False)
    block_ids = jnp.arange(vocab_size, dtype=jnp.int32)
    normed, root_mean = normalize(states[0], gain)
    width = head.shape[1]
    features = normed.shape[1]
    digits = digit_count(width * vocab_size)
    place = RADIX ** jnp.arange(digits, dtype=jnp.int32)
    shifts = RADIX_BITS * jnp.arange(digits, dtype=jnp.int32)
    coded = ((target_ids[0][:, None] >> shifts[None, :]) & (RADIX - 1)).astype(jnp.bfloat16)
    coded = jnp.pad(coded, ((0, 0), (0, LANES - digits)))
    packed = jnp.concatenate([normed, coded], axis=1)
    span = width // 2
    columns = lax.dynamic_slice_in_dim(head, core * span, span, 1)
    offset = vocab_index * width + core * span
    low_size = lax.axis_size("vocab_lo")
    high_size = lax.axis_size("vocab_hi")
    high_index = lax.axis_index("vocab_hi")
    near = lax.all_gather(packed, "vocab_lo", axis=0, tiled=True)
    swap = [(0, 1), (1, 0)]
    if high_size <= PIPELINE_LIMIT:
        far = [
            lax.ppermute(near, "vocab_hi", [(i, (i + shift) % high_size) for i in range(high_size)])
            for shift in range(1, high_size)
        ]
        near_rows = jnp.concatenate([near, lax.ppermute(near, "grp_lo", swap)])
        near_stats = partial_stats(near_rows, columns, features, digits, place, offset)
        far_own = jnp.concatenate(far)
        far_rows = jnp.concatenate([far_own, lax.ppermute(far_own, "grp_lo", swap)])
        far_stats = partial_stats(far_rows, columns, features, digits, place, offset)
        near_count = near.shape[0]
        far_count = far_own.shape[0]
        positions = jnp.arange(vocab_size, dtype=jnp.int32)
        block_of = ((high_index - positions // low_size) % high_size) * low_size + positions % low_size
        terms = jnp.stack(
            [
                jnp.concatenate(
                    [
                        jnp.concatenate([near_stat[:near_count], far_stat[:far_count]]),
                        jnp.concatenate([near_stat[near_count:], far_stat[far_count:]]),
                    ]
                )
                for near_stat, far_stat in zip(near_stats, far_stats)
            ]
        ).reshape(4, 2, vocab_size, count)
    else:
        own_rows = lax.all_gather(near, "vocab_hi", axis=0, tiled=True)
        pair_rows = jnp.concatenate([own_rows, lax.ppermute(own_rows, "grp_lo", swap)])
        terms = jnp.stack(partial_stats(pair_rows, columns, features, digits, place, offset))
        terms = terms.reshape(4, 2, vocab_size, count)
        block_of = block_ids
    pair_order = lax.dynamic_slice_in_dim(order, pair_base, 2, 0)
    pair_order = jnp.where(core == 0, pair_order, pair_order[::-1])
    pair_order = jnp.take(pair_order, block_of, axis=1)
    route = (pair_order[:, None, :] == block_ids[None, :, None]).astype(jnp.float32)
    routed = jnp.einsum("cjs,kcsr->jckr", route, terms, precision=lax.Precision.HIGHEST)
    routed = jnp.where(core == 0, routed, routed[:, ::-1])
    group_ids = jnp.arange(2, dtype=jnp.int32)
    home = own_order[vocab_index]
    root_slot = (block_ids[:, None] == home) & (group_ids[None, :] == core)
    root_rows = jnp.where(root_slot[:, :, None], root_mean[None, None, :], 0.0)
    payload = jnp.concatenate([routed, root_rows[:, :, None, :]], axis=2)
    payload = payload.reshape(vocab_size * 2, 5, count)
    received = lax.all_to_all(payload, VOCAB + ("grp_lo",), 0, 0, tiled=True)
    shard_max, shard_sums, shard_expected, shard_target, shard_root = (
        received[:, 0], received[:, 1], received[:, 2], received[:, 3], received[:, 4]
    )
    peak = jnp.max(shard_max, axis=0)
    scale = jnp.exp(shard_max - peak[None, :])
    totals = jnp.sum(shard_sums * scale, axis=0)
    own_expected = jnp.sum(shard_expected * scale, axis=0)
    own_target = jnp.sum(shard_target, axis=0)
    own_root = jnp.sum(shard_root, axis=0)
    source_block = jnp.sum(jnp.where(own_order == vocab_index, block_ids, 0))
    length_own = jnp.sum(jnp.where(block_ids == source_block, lengths[0], 0))
    keep = (jnp.arange(count, dtype=jnp.int32) < length_own).astype(jnp.float32)
    log_total = jnp.log(totals)
    log_prob = (own_target - peak - log_total) * keep
    entropy = (peak + log_total - own_expected / totals) * keep
    return (log_prob[None], entropy[None], (own_root * keep)[None], (peak * keep)[None])


def solution(mesh):
    vocab_size, group_size = mesh.devices.shape
    assert vocab_size % 2 == 0 and group_size % 2 == 0
    split = Mesh(mesh.devices.reshape(vocab_size // 2, 2, group_size // 2, 2), VOCAB + GROUP)
    in_specs = (
        P(GROUP, VOCAB, None),
        P(GROUP, VOCAB),
        P(GROUP, None),
        P(),
        P(),
        P(None, VOCAB),
    )
    out_specs = (P(GROUP, VOCAB),) * 4
    return jax.shard_map(shards, mesh=split, in_specs=in_specs, out_specs=out_specs, check_vma=False)
```

```python
import jax
import jax.numpy as jnp
from jax import lax
from jax.sharding import Mesh, PartitionSpec as P

EPSILON = 1e-05
RADIX_BITS = 8
RADIX = 1 << RADIX_BITS
VOCAB = ("vocab_hi", "vocab_lo")
GROUP = ("grp_hi", "grp_lo")
LANES = 128


def digit_count(total):
    digits = 1
    while RADIX**digits < total:
        digits += 1
    return digits


def normalize(block_states, gain):
    values = block_states.astype(jnp.float32)
    mean_square = jnp.mean(values * values, axis=-1)
    normed = (values * lax.rsqrt(mean_square + EPSILON)[:, None] * gain).astype(jnp.bfloat16)
    return (normed, jnp.sqrt(mean_square))


def partial_stats(normed, columns, token_ids, offset):
    logits = jnp.dot(normed, columns, preferred_element_type=jnp.float32)
    local_max = jnp.max(logits, axis=1)
    weights = jnp.exp(logits - local_max[:, None])
    within = token_ids - offset
    column = lax.broadcasted_iota(jnp.int32, logits.shape, 1)
    return (
        local_max,
        jnp.sum(weights, axis=1),
        jnp.sum(weights * logits, axis=1),
        jnp.sum(jnp.where(column == within[:, None], logits, 0.0), axis=1),
    )


def shards(states, target_ids, lengths, order, gain, head):
    count = states.shape[1]
    vocab_size = lax.axis_size(VOCAB)
    group_size = lax.axis_size(GROUP)
    vocab_index = lax.axis_index(VOCAB)
    group_index = lax.axis_index(GROUP)
    core = group_index % 2
    pair_base = group_index - core
    own_order = lax.dynamic_index_in_dim(order, group_index, 0, keepdims=False)
    block_ids = jnp.arange(vocab_size, dtype=jnp.int32)
    normed, root_mean = normalize(states[0], gain)
    width = head.shape[1]
    features = normed.shape[1]
    digits = digit_count(width * vocab_size)
    place = RADIX ** jnp.arange(digits, dtype=jnp.int32)
    shifts = RADIX_BITS * jnp.arange(digits, dtype=jnp.int32)
    coded = ((target_ids[0][:, None] >> shifts[None, :]) & (RADIX - 1)).astype(jnp.bfloat16)
    coded = jnp.pad(coded, ((0, 0), (0, LANES - digits)))
    packed = jnp.concatenate([normed, coded], axis=1)
    packed = lax.all_gather(packed, "vocab_lo", axis=0, tiled=True)
    packed = lax.all_gather(packed, "vocab_hi", axis=0, tiled=True)
    pair_rows = lax.all_gather(packed, "grp_lo", axis=0, tiled=True)
    pair_normed = pair_rows[:, :features]
    pair_ids = jnp.sum(pair_rows[:, features : features + digits].astype(jnp.int32) * place[None, :], axis=1)
    span = width // 2
    columns = lax.dynamic_slice_in_dim(head, core * span, span, 1)
    offset = vocab_index * width + core * span
    local_max, sums, expected, target = partial_stats(pair_normed, columns, pair_ids, offset)
    terms = jnp.stack([local_max, sums, expected, target]).reshape(4, 2, vocab_size, count)
    pair_order = lax.dynamic_slice_in_dim(order, pair_base, 2, 0)
    route = (pair_order[:, None, :] == block_ids[None, :, None]).astype(jnp.float32)
    routed = jnp.einsum("cjs,kcsr->jckr", route, terms, precision=lax.Precision.HIGHEST)
    group_ids = jnp.arange(2, dtype=jnp.int32)
    home = own_order[vocab_index]
    root_slot = (block_ids[:, None] == home) & (group_ids[None, :] == core)
    root_rows = jnp.where(root_slot[:, :, None], root_mean[None, None, :], 0.0)
    payload = jnp.concatenate([routed, root_rows[:, :, None, :]], axis=2)
    payload = payload.reshape(vocab_size * 2, 5, count)
    received = lax.all_to_all(payload, VOCAB + ("grp_lo",), 0, 0, tiled=True)
    shard_max, shard_sums, shard_expected, shard_target, shard_root = (
        received[:, 0], received[:, 1], received[:, 2], received[:, 3], received[:, 4]
    )
    peak = jnp.max(shard_max, axis=0)
    scale = jnp.exp(shard_max - peak[None, :])
    totals = jnp.sum(shard_sums * scale, axis=0)
    own_expected = jnp.sum(shard_expected * scale, axis=0)
    own_target = jnp.sum(shard_target, axis=0)
    own_root = jnp.sum(shard_root, axis=0)
    source_block = jnp.sum(jnp.where(own_order == vocab_index, block_ids, 0))
    length_own = jnp.sum(jnp.where(block_ids == source_block, lengths[0], 0))
    keep = (jnp.arange(count, dtype=jnp.int32) < length_own).astype(jnp.float32)
    log_total = jnp.log(totals)
    log_prob = (own_target - peak - log_total) * keep
    entropy = (peak + log_total - own_expected / totals) * keep
    return (log_prob[None], entropy[None], (own_root * keep)[None], (peak * keep)[None])


def solution(mesh):
    vocab_size, group_size = mesh.devices.shape
    assert vocab_size % 2 == 0 and group_size % 2 == 0
    split = Mesh(mesh.devices.reshape(vocab_size // 2, 2, group_size // 2, 2), VOCAB + GROUP)
    in_specs = (
        P(GROUP, VOCAB, None),
        P(GROUP, VOCAB),
        P(GROUP, None),
        P(),
        P(),
        P(None, VOCAB),
    )
    out_specs = (P(GROUP, VOCAB),) * 4
    return jax.shard_map(shards, mesh=split, in_specs=in_specs, out_specs=out_specs, check_vma=False)
```

```python
import jax
import jax.numpy as jnp
from jax import lax
from jax.sharding import Mesh, PartitionSpec as P

EPSILON = 1e-05
RADIX_BITS = 8
RADIX = 1 << RADIX_BITS
VOCAB = ("vocab_hi", "vocab_lo")
GROUP = ("grp_hi", "grp_lo")
LANES = 128


def digit_count(total):
    digits = 1
    while RADIX**digits < total:
        digits += 1
    return digits


def normalize(block_states, gain):
    values = block_states.astype(jnp.float32)
    mean_square = jnp.mean(values * values, axis=-1)
    normed = (values * lax.rsqrt(mean_square + EPSILON)[:, None] * gain).astype(jnp.bfloat16)
    return (normed, jnp.sqrt(mean_square))


def partial_stats(normed, columns, token_ids, offset):
    logits = jnp.dot(normed, columns, preferred_element_type=jnp.float32)
    local_max = jnp.max(logits, axis=1)
    weights = jnp.exp(logits - local_max[:, None])
    within = token_ids - offset
    column = lax.broadcasted_iota(jnp.int32, logits.shape, 1)
    return (
        local_max,
        jnp.sum(weights, axis=1),
        jnp.sum(weights * logits, axis=1),
        jnp.sum(jnp.where(column == within[:, None], logits, 0.0), axis=1),
    )


def shards(states, target_ids, lengths, order, gain, head):
    count = states.shape[1]
    vocab_size = lax.axis_size(VOCAB)
    group_size = lax.axis_size(GROUP)
    vocab_index = lax.axis_index(VOCAB)
    group_index = lax.axis_index(GROUP)
    core = group_index % 2
    pair_base = group_index - core
    own_order = lax.dynamic_index_in_dim(order, group_index, 0, keepdims=False)
    block_ids = jnp.arange(vocab_size, dtype=jnp.int32)
    normed, root_mean = normalize(states[0], gain)
    width = head.shape[1]
    features = normed.shape[1]
    digits = digit_count(width * vocab_size)
    place = RADIX ** jnp.arange(digits, dtype=jnp.int32)
    shifts = RADIX_BITS * jnp.arange(digits, dtype=jnp.int32)
    coded = ((target_ids[0][:, None] >> shifts[None, :]) & (RADIX - 1)).astype(jnp.bfloat16)
    coded = jnp.pad(coded, ((0, 0), (0, LANES - digits)))
    packed = jnp.concatenate([normed, coded], axis=1)
    low_index = lax.axis_index("vocab_lo")
    if lax.axis_size("vocab_lo") == 2:
        packed = jnp.concatenate([packed, lax.ppermute(packed, "vocab_lo", [(0, 1), (1, 0)])])
        positions = jnp.arange(vocab_size, dtype=jnp.int32)
        block_of = (positions // 2) * 2 + ((positions % 2) ^ low_index)
    else:
        packed = lax.all_gather(packed, "vocab_lo", axis=0, tiled=True)
        block_of = block_ids
    packed = lax.all_gather(packed, "vocab_hi", axis=0, tiled=True)
    partner = lax.ppermute(packed, "grp_lo", [(0, 1), (1, 0)])
    pair_rows = jnp.where(core == 0, jnp.concatenate([packed, partner]), jnp.concatenate([partner, packed]))
    pair_normed = pair_rows[:, :features]
    pair_ids = jnp.sum(pair_rows[:, features : features + digits].astype(jnp.int32) * place[None, :], axis=1)
    span = width // 2
    columns = lax.dynamic_slice_in_dim(head, core * span, span, 1)
    offset = vocab_index * width + core * span
    local_max, sums, expected, target = partial_stats(pair_normed, columns, pair_ids, offset)
    terms = jnp.stack([local_max, sums, expected, target]).reshape(4, 2, vocab_size, count)
    pair_order = lax.dynamic_slice_in_dim(order, pair_base, 2, 0)
    pair_order = jnp.take(pair_order, block_of, axis=1)
    route = (pair_order[:, None, :] == block_ids[None, :, None]).astype(jnp.float32)
    routed = jnp.einsum("cjs,kcsr->jckr", route, terms, precision=lax.Precision.HIGHEST)
    group_ids = jnp.arange(2, dtype=jnp.int32)
    home = own_order[vocab_index]
    root_slot = (block_ids[:, None] == home) & (group_ids[None, :] == core)
    root_rows = jnp.where(root_slot[:, :, None], root_mean[None, None, :], 0.0)
    payload = jnp.concatenate([routed, root_rows[:, :, None, :]], axis=2)
    payload = payload.reshape(vocab_size * 2, 5, count)
    received = lax.all_to_all(payload, VOCAB + ("grp_lo",), 0, 0, tiled=True)
    shard_max, shard_sums, shard_expected, shard_target, shard_root = (
        received[:, 0], received[:, 1], received[:, 2], received[:, 3], received[:, 4]
    )
    peak = jnp.max(shard_max, axis=0)
    scale = jnp.exp(shard_max - peak[None, :])
    totals = jnp.sum(shard_sums * scale, axis=0)
    own_expected = jnp.sum(shard_expected * scale, axis=0)
    own_target = jnp.sum(shard_target, axis=0)
    own_root = jnp.sum(shard_root, axis=0)
    source_block = jnp.sum(jnp.where(own_order == vocab_index, block_ids, 0))
    length_own = jnp.sum(jnp.where(block_ids == source_block, lengths[0], 0))
    keep = (jnp.arange(count, dtype=jnp.int32) < length_own).astype(jnp.float32)
    log_total = jnp.log(totals)
    log_prob = (own_target - peak - log_total) * keep
    entropy = (peak + log_total - own_expected / totals) * keep
    return (log_prob[None], entropy[None], (own_root * keep)[None], (peak * keep)[None])


def solution(mesh):
    vocab_size, group_size = mesh.devices.shape
    assert vocab_size % 2 == 0 and group_size % 2 == 0
    split = Mesh(mesh.devices.reshape(vocab_size // 2, 2, group_size // 2, 2), VOCAB + GROUP)
    in_specs = (
        P(GROUP, VOCAB, None),
        P(GROUP, VOCAB),
        P(GROUP, None),
        P(),
        P(),
        P(None, VOCAB),
    )
    out_specs = (P(GROUP, VOCAB),) * 4
    return jax.shard_map(shards, mesh=split, in_specs=in_specs, out_specs=out_specs, check_vma=False)
```

```python
from functools import partial

import jax
import jax.numpy as jnp
from jax import lax
from jax.experimental import pallas as pl
from jax.sharding import Mesh, PartitionSpec as P

EPSILON = 1e-05
RADIX_BITS = 8
RADIX = 1 << RADIX_BITS
VOCAB = ("vocab_hi", "vocab_lo")
GROUP = ("grp_hi", "grp_lo")
LANES = 128


def digit_count(total):
    digits = 1
    while RADIX**digits < total:
        digits += 1
    return digits


def normalize(block_states, gain):
    values = block_states.astype(jnp.float32)
    mean_square = jnp.mean(values * values, axis=-1)
    normed = (values * lax.rsqrt(mean_square + EPSILON)[:, None] * gain).astype(jnp.bfloat16)
    return (normed, jnp.sqrt(mean_square))


def partial_stats(normed, columns, token_ids, offset):
    logits = jnp.dot(normed, columns, preferred_element_type=jnp.float32)
    local_max = jnp.max(logits, axis=1)
    weights = jnp.exp(logits - local_max[:, None])
    within = token_ids - offset
    column = lax.broadcasted_iota(jnp.int32, logits.shape, 1)
    return (
        local_max,
        jnp.sum(weights, axis=1),
        jnp.sum(weights * logits, axis=1),
        jnp.sum(jnp.where(column == within[:, None], logits, 0.0), axis=1),
    )


def pack_kernel(states_ref, gain_ref, ids_ref, out_ref, *, features, digits):
    values = states_ref[...].astype(jnp.float32)
    mean_square = jnp.mean(values * values, axis=1, keepdims=True)
    normed = (values * lax.rsqrt(mean_square + EPSILON) * gain_ref[...]).astype(jnp.bfloat16)
    out_ref[:, :features] = normed
    ids = ids_ref[...]
    count = ids.shape[1]
    row = lax.broadcasted_iota(jnp.int32, (count, count), 0)
    col = lax.broadcasted_iota(jnp.int32, (count, count), 1)
    token = jnp.sum(jnp.where(row == col, jnp.broadcast_to(ids, (count, count)), 0), axis=1, keepdims=True)
    lane = lax.broadcasted_iota(jnp.int32, (count, LANES), 1)
    code = jnp.zeros((count, LANES), jnp.int32)
    for k in range(digits):
        code = jnp.where(lane == k, (token >> (RADIX_BITS * k)) & (RADIX - 1), code)
    out_ref[:, features:] = code.astype(jnp.float32).astype(jnp.bfloat16)


def pack_rows(block_states, gain, token_ids, digits):
    count, features = block_states.shape
    return pl.pallas_call(
        partial(pack_kernel, features=features, digits=digits),
        out_shape=jax.ShapeDtypeStruct((count, features + LANES), jnp.bfloat16),
    )(block_states, gain.reshape(1, features), token_ids)


def shards(states, target_ids, lengths, order, gain, head):
    count = states.shape[1]
    vocab_size = lax.axis_size(VOCAB)
    group_size = lax.axis_size(GROUP)
    vocab_index = lax.axis_index(VOCAB)
    group_index = lax.axis_index(GROUP)
    core = group_index % 2
    pair_base = group_index - core
    own_order = lax.dynamic_index_in_dim(order, group_index, 0, keepdims=False)
    block_ids = jnp.arange(vocab_size, dtype=jnp.int32)
    root_mean = jnp.sqrt(jnp.mean(jnp.square(states[0].astype(jnp.float32)), axis=-1))
    width = head.shape[1]
    features = states.shape[2]
    digits = digit_count(width * vocab_size)
    packed = pack_rows(states[0], gain, target_ids, digits)
    low_index = lax.axis_index("vocab_lo")
    if lax.axis_size("vocab_lo") == 2:
        packed = jnp.concatenate([packed, lax.ppermute(packed, "vocab_lo", [(0, 1), (1, 0)])])
        positions = jnp.arange(vocab_size, dtype=jnp.int32)
        block_of = (positions // 2) * 2 + ((positions % 2) ^ low_index)
    else:
        packed = lax.all_gather(packed, "vocab_lo", axis=0, tiled=True)
        block_of = block_ids
    packed = lax.all_gather(packed, "vocab_hi", axis=0, tiled=True)
    partner = lax.ppermute(packed, "grp_lo", [(0, 1), (1, 0)])
    pair_rows = jnp.where(core == 0, jnp.concatenate([packed, partner]), jnp.concatenate([partner, packed]))
    pair_normed = pair_rows[:, :features]
    pair_ids = pair_rows[:, features].astype(jnp.int32)
    for k in range(1, digits):
        pair_ids = pair_ids + (pair_rows[:, features + k].astype(jnp.int32) << (RADIX_BITS * k))
    span = width // 2
    columns = lax.dynamic_slice_in_dim(head, core * span, span, 1)
    offset = vocab_index * width + core * span
    local_max, sums, expected, target = partial_stats(pair_normed, columns, pair_ids, offset)
    terms = jnp.stack([local_max, sums, expected, target]).reshape(4, 2, vocab_size, count)
    pair_order = lax.dynamic_slice_in_dim(order, pair_base, 2, 0)
    pair_order = jnp.take(pair_order, block_of, axis=1)
    route = (pair_order[:, None, :] == block_ids[None, :, None]).astype(jnp.float32)
    routed = jnp.einsum("cjs,kcsr->jckr", route, terms, precision=lax.Precision.HIGHEST)
    group_ids = jnp.arange(2, dtype=jnp.int32)
    home = own_order[vocab_index]
    root_slot = (block_ids[:, None] == home) & (group_ids[None, :] == core)
    root_rows = jnp.where(root_slot[:, :, None], root_mean[None, None, :], 0.0)
    payload = jnp.concatenate([routed, root_rows[:, :, None, :]], axis=2)
    payload = payload.reshape(vocab_size * 2, 5, count)
    received = lax.all_to_all(payload, VOCAB + ("grp_lo",), 0, 0, tiled=True)
    shard_max, shard_sums, shard_expected, shard_target, shard_root = (
        received[:, 0], received[:, 1], received[:, 2], received[:, 3], received[:, 4]
    )
    peak = jnp.max(shard_max, axis=0)
    scale = jnp.exp(shard_max - peak[None, :])
    totals = jnp.sum(shard_sums * scale, axis=0)
    own_expected = jnp.sum(shard_expected * scale, axis=0)
    own_target = jnp.sum(shard_target, axis=0)
    own_root = jnp.sum(shard_root, axis=0)
    source_block = jnp.sum(jnp.where(own_order == vocab_index, block_ids, 0))
    length_own = jnp.sum(jnp.where(block_ids == source_block, lengths[0], 0))
    keep = (jnp.arange(count, dtype=jnp.int32) < length_own).astype(jnp.float32)
    log_total = jnp.log(totals)
    log_prob = (own_target - peak - log_total) * keep
    entropy = (peak + log_total - own_expected / totals) * keep
    return (log_prob[None], entropy[None], (own_root * keep)[None], (peak * keep)[None])


def solution(mesh):
    vocab_size, group_size = mesh.devices.shape
    assert vocab_size % 2 == 0 and group_size % 2 == 0
    split = Mesh(mesh.devices.reshape(vocab_size // 2, 2, group_size // 2, 2), VOCAB + GROUP)
    in_specs = (
        P(GROUP, VOCAB, None),
        P(GROUP, VOCAB),
        P(GROUP, None),
        P(),
        P(),
        P(None, VOCAB),
    )
    out_specs = (P(GROUP, VOCAB),) * 4
    return jax.shard_map(shards, mesh=split, in_specs=in_specs, out_specs=out_specs, check_vma=False)
```

```python
import jax
import jax.numpy as jnp
from jax import lax
from jax.sharding import Mesh, PartitionSpec as P

EPSILON = 1e-05
RADIX_BITS = 8
RADIX = 1 << RADIX_BITS
VOCAB = ("vocab_hi", "vocab_lo")
GROUP = ("grp_hi", "grp_lo")
LANES = 128


def digit_count(total):
    digits = 1
    while RADIX**digits < total:
        digits += 1
    return digits


def normalize(block_states, gain):
    values = block_states.astype(jnp.float32)
    mean_square = jnp.mean(values * values, axis=-1)
    normed = (values * lax.rsqrt(mean_square + EPSILON)[:, None] * gain).astype(jnp.bfloat16)
    return (normed, jnp.sqrt(mean_square))


def partial_stats(normed, columns, token_ids, offset):
    logits = jnp.dot(normed, columns, preferred_element_type=jnp.float32)
    local_max = jnp.max(logits, axis=1)
    weights = jnp.exp(logits - local_max[:, None])
    within = token_ids - offset
    column = lax.broadcasted_iota(jnp.int32, logits.shape, 1)
    return (
        local_max,
        jnp.sum(weights, axis=1),
        jnp.sum(weights * logits, axis=1),
        jnp.sum(jnp.where(column == within[:, None], logits, 0.0), axis=1),
    )


def shards(states, target_ids, lengths, order, gain, head):
    count = states.shape[1]
    vocab_size = lax.axis_size(VOCAB)
    group_size = lax.axis_size(GROUP)
    vocab_index = lax.axis_index(VOCAB)
    group_index = lax.axis_index(GROUP)
    core = group_index % 2
    pair_base = group_index - core
    own_order = lax.dynamic_index_in_dim(order, group_index, 0, keepdims=False)
    block_ids = jnp.arange(vocab_size, dtype=jnp.int32)
    normed, root_mean = normalize(states[0], gain)
    width = head.shape[1]
    features = normed.shape[1]
    digits = digit_count(width * vocab_size)
    place = RADIX ** jnp.arange(digits, dtype=jnp.int32)
    shifts = RADIX_BITS * jnp.arange(digits, dtype=jnp.int32)
    coded = ((target_ids[0][:, None] >> shifts[None, :]) & (RADIX - 1)).astype(jnp.bfloat16)
    coded = jnp.pad(coded, ((0, 0), (0, LANES - digits)))
    packed = jnp.concatenate([normed, coded], axis=1)
    low_index = lax.axis_index("vocab_lo")
    if lax.axis_size("vocab_lo") == 2:
        packed = jnp.concatenate([packed, lax.ppermute(packed, "vocab_lo", [(0, 1), (1, 0)])])
        positions = jnp.arange(vocab_size, dtype=jnp.int32)
        block_of = (positions // 2) * 2 + ((positions % 2) ^ low_index)
    else:
        packed = lax.all_gather(packed, "vocab_lo", axis=0, tiled=True)
        block_of = block_ids
    packed = lax.all_gather(packed, "vocab_hi", axis=0, tiled=True)
    partner = lax.ppermute(packed, "grp_lo", [(0, 1), (1, 0)])
    pair_rows = jnp.where(core == 0, jnp.concatenate([packed, partner]), jnp.concatenate([partner, packed]))
    pair_normed = pair_rows[:, :features]
    pair_ids = jnp.sum(pair_rows[:, features : features + digits].astype(jnp.int32) * place[None, :], axis=1)
    span = width // 2
    columns = lax.dynamic_slice_in_dim(head, core * span, span, 1)
    offset = vocab_index * width + core * span
    local_max, sums, expected, target = partial_stats(pair_normed, columns, pair_ids, offset)
    own_block = (block_of[:, None] == vocab_index).astype(jnp.float32) * root_mean[None, :]
    blank = jnp.zeros_like(own_block)
    root_terms = jnp.where(
        core == 0, jnp.concatenate([own_block, blank]), jnp.concatenate([blank, own_block])
    ).reshape(-1)
    terms = jnp.stack([local_max, sums, expected, target, root_terms]).reshape(5, 2, vocab_size, count)
    pair_order = lax.dynamic_slice_in_dim(order, pair_base, 2, 0)
    pair_order = jnp.take(pair_order, block_of, axis=1)
    route = (pair_order[:, None, :] == block_ids[None, :, None]).astype(jnp.float32)
    routed = jnp.einsum("cjs,kcsr->cjkr", route, terms, precision=lax.Precision.HIGHEST)
    payload = routed.reshape(2 * vocab_size, 5, count)
    received = lax.all_to_all(payload, ("grp_lo",) + VOCAB, 0, 0, tiled=True)
    shard_max, shard_sums, shard_expected, shard_target, shard_root = (
        received[:, 0], received[:, 1], received[:, 2], received[:, 3], received[:, 4]
    )
    peak = jnp.max(shard_max, axis=0)
    scale = jnp.exp(shard_max - peak[None, :])
    totals = jnp.sum(shard_sums * scale, axis=0)
    own_expected = jnp.sum(shard_expected * scale, axis=0)
    own_target = jnp.sum(shard_target, axis=0)
    own_root = jnp.sum(shard_root, axis=0)
    source_block = jnp.sum(jnp.where(own_order == vocab_index, block_ids, 0))
    length_own = jnp.sum(jnp.where(block_ids == source_block, lengths[0], 0))
    keep = (jnp.arange(count, dtype=jnp.int32) < length_own).astype(jnp.float32)
    log_total = jnp.log(totals)
    log_prob = (own_target - peak - log_total) * keep
    entropy = (peak + log_total - own_expected / totals) * keep
    return (log_prob[None], entropy[None], (own_root * keep)[None], (peak * keep)[None])


def solution(mesh):
    vocab_size, group_size = mesh.devices.shape
    assert vocab_size % 2 == 0 and group_size % 2 == 0
    split = Mesh(mesh.devices.reshape(vocab_size // 2, 2, group_size // 2, 2), VOCAB + GROUP)
    in_specs = (
        P(GROUP, VOCAB, None),
        P(GROUP, VOCAB),
        P(GROUP, None),
        P(),
        P(),
        P(None, VOCAB),
    )
    out_specs = (P(GROUP, VOCAB),) * 4
    return jax.shard_map(shards, mesh=split, in_specs=in_specs, out_specs=out_specs, check_vma=False)
```

```python
import jax
import jax.numpy as jnp
from jax import lax
from jax.sharding import Mesh, PartitionSpec as P

EPSILON = 1e-05
RADIX_BITS = 8
RADIX = 1 << RADIX_BITS
VOCAB = ("vocab_hi", "vocab_lo")
GROUP = ("grp_hi", "grp_lo")
LANES = 128


def digit_count(total):
    digits = 1
    while RADIX**digits < total:
        digits += 1
    return digits


def normalize(block_states, gain):
    values = block_states.astype(jnp.float32)
    mean_square = jnp.mean(values * values, axis=-1)
    normed = (values * lax.rsqrt(mean_square + EPSILON)[:, None] * gain).astype(jnp.bfloat16)
    return (normed, jnp.sqrt(mean_square))


def partial_stats(normed, columns, token_ids, offset):
    logits = jnp.dot(normed, columns, preferred_element_type=jnp.float32)
    local_max = jnp.max(logits, axis=1)
    weights = jnp.exp(logits - local_max[:, None])
    within = token_ids - offset
    column = lax.broadcasted_iota(jnp.int32, logits.shape, 1)
    return (
        local_max,
        jnp.sum(weights, axis=1),
        jnp.sum(weights * logits, axis=1),
        jnp.sum(jnp.where(column == within[:, None], logits, 0.0), axis=1),
    )


def shards(states, target_ids, lengths, order, gain, head):
    count = states.shape[1]
    vocab_size = lax.axis_size(VOCAB)
    group_size = lax.axis_size(GROUP)
    vocab_index = lax.axis_index(VOCAB)
    group_index = lax.axis_index(GROUP)
    core = group_index % 2
    pair_base = group_index - core
    own_order = lax.dynamic_index_in_dim(order, group_index, 0, keepdims=False)
    block_ids = jnp.arange(vocab_size, dtype=jnp.int32)
    normed, root_mean = normalize(states[0], gain)
    width = head.shape[1]
    features = normed.shape[1]
    digits = digit_count(width * vocab_size)
    place = RADIX ** jnp.arange(digits, dtype=jnp.int32)
    shifts = RADIX_BITS * jnp.arange(digits, dtype=jnp.int32)
    coded = ((target_ids[0][:, None] >> shifts[None, :]) & (RADIX - 1)).astype(jnp.bfloat16)
    coded = jnp.pad(coded, ((0, 0), (0, LANES - digits)))
    packed = jnp.concatenate([normed, coded], axis=1)
    low_index = lax.axis_index("vocab_lo")
    if lax.axis_size("vocab_lo") == 2:
        packed = jnp.concatenate([packed, lax.ppermute(packed, "vocab_lo", [(0, 1), (1, 0)])])
        positions = jnp.arange(vocab_size, dtype=jnp.int32)
        block_of = (positions // 2) * 2 + ((positions % 2) ^ low_index)
    else:
        packed = lax.all_gather(packed, "vocab_lo", axis=0, tiled=True)
        block_of = block_ids
    packed = lax.all_gather(packed, "vocab_hi", axis=0, tiled=True)
    partner = lax.ppermute(packed, "grp_lo", [(0, 1), (1, 0)])
    pair_rows = jnp.where(core == 0, jnp.concatenate([packed, partner]), jnp.concatenate([partner, packed]))
    pair_normed = pair_rows[:, :features]
    pair_ids = jnp.sum(pair_rows[:, features : features + digits].astype(jnp.int32) * place[None, :], axis=1)
    span = width // 2
    columns = lax.dynamic_slice_in_dim(head, core * span, span, 1)
    offset = vocab_index * width + core * span
    local_max, sums, expected, target = partial_stats(pair_normed, columns, pair_ids, offset)
    own_length = lax.dynamic_index_in_dim(lengths[0], vocab_index, 0, keepdims=False)
    own_keep = (jnp.arange(count, dtype=jnp.int32) < own_length).astype(jnp.float32)
    at_home = (block_of[:, None] == vocab_index).astype(jnp.float32)
    blank = jnp.zeros((vocab_size, count), jnp.float32)

    def home_term(values):
        own_block = at_home * values[None, :]
        return jnp.where(
            core == 0, jnp.concatenate([own_block, blank]), jnp.concatenate([blank, own_block])
        ).reshape(-1)

    terms = jnp.stack([local_max, sums, expected, target, home_term(root_mean), home_term(own_keep)])
    terms = terms.reshape(6, 2, vocab_size, count)
    pair_order = lax.dynamic_slice_in_dim(order, pair_base, 2, 0)
    pair_order = jnp.take(pair_order, block_of, axis=1)
    route = (pair_order[:, None, :] == block_ids[None, :, None]).astype(jnp.float32)
    routed = jnp.einsum("cjs,kcsr->cjkr", route, terms, precision=lax.Precision.HIGHEST)
    payload = routed.reshape(2 * vocab_size, 6, count)
    received = lax.all_to_all(payload, ("grp_lo",) + VOCAB, 0, 0, tiled=True)
    shard_max, shard_sums, shard_expected, shard_target, shard_root, shard_keep = (
        received[:, k] for k in range(6)
    )
    peak = jnp.max(shard_max, axis=0)
    scale = jnp.exp(shard_max - peak[None, :])
    totals = jnp.sum(shard_sums * scale, axis=0)
    own_expected = jnp.sum(shard_expected * scale, axis=0)
    own_target = jnp.sum(shard_target, axis=0)
    own_root = jnp.sum(shard_root, axis=0)
    keep = jnp.sum(shard_keep, axis=0)
    log_total = jnp.log(totals)
    log_prob = (own_target - peak - log_total) * keep
    entropy = (peak + log_total - own_expected / totals) * keep
    return (log_prob[None], entropy[None], (own_root * keep)[None], (peak * keep)[None])


def solution(mesh):
    vocab_size, group_size = mesh.devices.shape
    assert vocab_size % 2 == 0 and group_size % 2 == 0
    split = Mesh(mesh.devices.reshape(vocab_size // 2, 2, group_size // 2, 2), VOCAB + GROUP)
    in_specs = (
        P(GROUP, VOCAB, None),
        P(GROUP, VOCAB),
        P(GROUP, None),
        P(),
        P(),
        P(None, VOCAB),
    )
    out_specs = (P(GROUP, VOCAB),) * 4
    return jax.shard_map(shards, mesh=split, in_specs=in_specs, out_specs=out_specs, check_vma=False)
```

```python
import jax
import jax.numpy as jnp
from jax import lax
from jax.sharding import Mesh, PartitionSpec as P

EPSILON = 1e-05
RADIX_BITS = 8
RADIX = 1 << RADIX_BITS
VOCAB = ("vocab_hi", "vocab_lo")
GROUP = ("grp_hi", "grp_lo")
LANES = 128


def digit_count(total):
    digits = 1
    while RADIX**digits < total:
        digits += 1
    return digits


def normalize(block_states, gain):
    values = block_states.astype(jnp.float32)
    mean_square = jnp.mean(values * values, axis=-1)
    normed = (values * lax.rsqrt(mean_square + EPSILON)[:, None] * gain).astype(jnp.bfloat16)
    return (normed, jnp.sqrt(mean_square))


def partial_stats(normed, columns, token_ids, offset):
    logits = jnp.dot(normed, columns, preferred_element_type=jnp.float32)
    local_max = jnp.max(logits, axis=1)
    weights = jnp.exp(logits - local_max[:, None])
    within = token_ids - offset
    column = lax.broadcasted_iota(jnp.int32, logits.shape, 1)
    return (
        local_max,
        jnp.sum(weights, axis=1),
        jnp.sum(weights * logits, axis=1),
        jnp.sum(jnp.where(column == within[:, None], logits, 0.0), axis=1),
    )


def shards(states, target_ids, lengths, order, gain, head):
    count = states.shape[1]
    vocab_size = lax.axis_size(VOCAB)
    group_size = lax.axis_size(GROUP)
    vocab_index = lax.axis_index(VOCAB)
    group_index = lax.axis_index(GROUP)
    core = group_index % 2
    pair_base = group_index - core
    own_order = lax.dynamic_index_in_dim(order, group_index, 0, keepdims=False)
    block_ids = jnp.arange(vocab_size, dtype=jnp.int32)
    normed, root_mean = normalize(states[0], gain)
    width = head.shape[1]
    features = normed.shape[1]
    digits = digit_count(width * vocab_size)
    place = RADIX ** jnp.arange(digits, dtype=jnp.int32)
    shifts = RADIX_BITS * jnp.arange(digits, dtype=jnp.int32)
    coded = ((target_ids[0][:, None] >> shifts[None, :]) & (RADIX - 1)).astype(jnp.bfloat16)
    coded = jnp.pad(coded, ((0, 0), (0, LANES - digits)))
    packed = jnp.concatenate([normed, coded], axis=1)
    low_index = lax.axis_index("vocab_lo")
    if lax.axis_size("vocab_lo") == 2:
        positions = jnp.arange(vocab_size, dtype=jnp.int32)
        block_of = (positions // 2) * 2 + ((positions % 2) ^ low_index)
        received_low = lax.ppermute(packed, "vocab_lo", [(0, 1), (1, 0)])
    else:
        block_of = block_ids
        received_low = packed
    pair_order = lax.dynamic_slice_in_dim(order, pair_base, 2, 0)
    pair_order = jnp.take(pair_order, block_of, axis=1)
    route = (pair_order[:, None, :] == block_ids[None, :, None]).astype(jnp.float32)
    own_length = lax.dynamic_index_in_dim(lengths[0], vocab_index, 0, keepdims=False)
    own_keep = (jnp.arange(count, dtype=jnp.int32) < own_length).astype(jnp.float32)
    route, own_keep, received_low = lax.optimization_barrier((route, own_keep, received_low))
    if lax.axis_size("vocab_lo") == 2:
        packed = jnp.concatenate([packed, received_low])
    else:
        packed = lax.all_gather(packed, "vocab_lo", axis=0, tiled=True)
    packed = lax.all_gather(packed, "vocab_hi", axis=0, tiled=True)
    partner = lax.ppermute(packed, "grp_lo", [(0, 1), (1, 0)])
    pair_rows = jnp.where(core == 0, jnp.concatenate([packed, partner]), jnp.concatenate([partner, packed]))
    pair_normed = pair_rows[:, :features]
    pair_ids = jnp.sum(pair_rows[:, features : features + digits].astype(jnp.int32) * place[None, :], axis=1)
    span = width // 2
    columns = lax.dynamic_slice_in_dim(head, core * span, span, 1)
    offset = vocab_index * width + core * span
    local_max, sums, expected, target = partial_stats(pair_normed, columns, pair_ids, offset)
    at_home = (block_of[:, None] == vocab_index).astype(jnp.float32)
    blank = jnp.zeros((vocab_size, count), jnp.float32)

    def home_term(values):
        own_block = at_home * values[None, :]
        return jnp.where(
            core == 0, jnp.concatenate([own_block, blank]), jnp.concatenate([blank, own_block])
        ).reshape(-1)

    terms = jnp.stack([local_max, sums, expected, target, home_term(root_mean), home_term(own_keep)])
    terms = terms.reshape(6, 2, vocab_size, count)
    routed = jnp.einsum("cjs,kcsr->cjkr", route, terms, precision=lax.Precision.HIGHEST)
    payload = routed.reshape(2 * vocab_size, 6, count)
    received = lax.all_to_all(payload, ("grp_lo",) + VOCAB, 0, 0, tiled=True)
    shard_max, shard_sums, shard_expected, shard_target, shard_root, shard_keep = (
        received[:, k] for k in range(6)
    )
    peak = jnp.max(shard_max, axis=0)
    scale = jnp.exp(shard_max - peak[None, :])
    totals = jnp.sum(shard_sums * scale, axis=0)
    own_expected = jnp.sum(shard_expected * scale, axis=0)
    own_target = jnp.sum(shard_target, axis=0)
    own_root = jnp.sum(shard_root, axis=0)
    keep = jnp.sum(shard_keep, axis=0)
    log_total = jnp.log(totals)
    log_prob = (own_target - peak - log_total) * keep
    entropy = (peak + log_total - own_expected / totals) * keep
    return (log_prob[None], entropy[None], (own_root * keep)[None], (peak * keep)[None])


def solution(mesh):
    vocab_size, group_size = mesh.devices.shape
    assert vocab_size % 2 == 0 and group_size % 2 == 0
    split = Mesh(mesh.devices.reshape(vocab_size // 2, 2, group_size // 2, 2), VOCAB + GROUP)
    in_specs = (
        P(GROUP, VOCAB, None),
        P(GROUP, VOCAB),
        P(GROUP, None),
        P(),
        P(),
        P(None, VOCAB),
    )
    out_specs = (P(GROUP, VOCAB),) * 4
    return jax.shard_map(shards, mesh=split, in_specs=in_specs, out_specs=out_specs, check_vma=False)
```

```python
import jax
import jax.numpy as jnp
from jax import lax
from jax.sharding import Mesh, PartitionSpec as P

EPSILON = 1e-05
RADIX_BITS = 8
RADIX = 1 << RADIX_BITS
VOCAB = ("vocab_hi", "vocab_lo")
GROUP = ("grp_hi", "grp_lo")
LANES = 128


def digit_count(total):
    digits = 1
    while RADIX**digits < total:
        digits += 1
    return digits


def normalize(block_states, gain):
    values = block_states.astype(jnp.float32)
    mean_square = jnp.mean(values * values, axis=-1)
    normed = (values * lax.rsqrt(mean_square + EPSILON)[:, None] * gain).astype(jnp.bfloat16)
    return (normed, jnp.sqrt(mean_square))


def partial_stats(normed, columns, token_ids, offset):
    logits = jnp.dot(normed, columns, preferred_element_type=jnp.float32)
    local_max = jnp.max(logits, axis=1)
    weights = jnp.exp(logits - local_max[:, None])
    within = token_ids - offset
    column = lax.broadcasted_iota(jnp.int32, logits.shape, 1)
    return (
        local_max,
        jnp.sum(weights, axis=1),
        jnp.sum(weights * logits, axis=1),
        jnp.sum(jnp.where(column == within[:, None], logits, 0.0), axis=1),
    )


def shards(states, target_ids, lengths, order, gain, head):
    count = states.shape[1]
    vocab_size = lax.axis_size(VOCAB)
    group_size = lax.axis_size(GROUP)
    vocab_index = lax.axis_index(VOCAB)
    group_index = lax.axis_index(GROUP)
    core = group_index % 2
    pair_base = group_index - core
    own_order = lax.dynamic_index_in_dim(order, group_index, 0, keepdims=False)
    block_ids = jnp.arange(vocab_size, dtype=jnp.int32)
    normed, root_mean = normalize(states[0], gain)
    width = head.shape[1]
    features = normed.shape[1]
    digits = digit_count(width * vocab_size)
    place = RADIX ** jnp.arange(digits, dtype=jnp.int32)
    shifts = RADIX_BITS * jnp.arange(digits, dtype=jnp.int32)
    coded = ((target_ids[0][:, None] >> shifts[None, :]) & (RADIX - 1)).astype(jnp.bfloat16)
    coded = jnp.pad(coded, ((0, 0), (0, LANES - digits)))
    packed = jnp.concatenate([normed, coded], axis=1)
    low_index = lax.axis_index("vocab_lo")
    if lax.axis_size("vocab_lo") == 2:
        positions = jnp.arange(vocab_size, dtype=jnp.int32)
        block_of = (positions // 2) * 2 + ((positions % 2) ^ low_index)
        received_low = lax.ppermute(packed, "vocab_lo", [(0, 1), (1, 0)])
    else:
        block_of = block_ids
        received_low = packed
    pair_order = lax.dynamic_slice_in_dim(order, pair_base, 2, 0)
    pair_order = jnp.take(pair_order, block_of, axis=1)
    route = (pair_order[:, None, :] == block_ids[None, :, None]).astype(jnp.float32)
    own_length = lax.dynamic_index_in_dim(lengths[0], vocab_index, 0, keepdims=False)
    own_keep = (jnp.arange(count, dtype=jnp.int32) < own_length).astype(jnp.float32)
    route, own_keep, received_low = lax.optimization_barrier((route, own_keep, received_low))
    if lax.axis_size("vocab_lo") == 2:
        packed = jnp.concatenate([packed, received_low])
    else:
        packed = lax.all_gather(packed, "vocab_lo", axis=0, tiled=True)
    packed = lax.all_gather(packed, "vocab_hi", axis=0, tiled=True)
    partner = lax.ppermute(packed, "grp_lo", [(0, 1), (1, 0)])
    pair_rows = jnp.where(core == 0, jnp.concatenate([packed, partner]), jnp.concatenate([partner, packed]))
    pair_normed = jnp.where(
        core == 0,
        jnp.concatenate([packed[:, :features], partner[:, :features]]),
        jnp.concatenate([partner[:, :features], packed[:, :features]]),
    )
    pair_ids = jnp.sum(pair_rows[:, features : features + digits].astype(jnp.int32) * place[None, :], axis=1)
    span = width // 2
    columns = lax.dynamic_slice_in_dim(head, core * span, span, 1)
    offset = vocab_index * width + core * span
    local_max, sums, expected, target = partial_stats(pair_normed, columns, pair_ids, offset)
    at_home = (block_of[:, None] == vocab_index).astype(jnp.float32)
    blank = jnp.zeros((vocab_size, count), jnp.float32)

    def home_term(values):
        own_block = at_home * values[None, :]
        return jnp.where(
            core == 0, jnp.concatenate([own_block, blank]), jnp.concatenate([blank, own_block])
        ).reshape(-1)

    terms = jnp.stack([local_max, sums, expected, target, home_term(root_mean), home_term(own_keep)])
    terms = terms.reshape(6, 2, vocab_size, count)
    routed = jnp.einsum("cjs,kcsr->cjkr", route, terms, precision=lax.Precision.HIGHEST)
    payload = routed.reshape(2 * vocab_size, 6, count)
    received = lax.all_to_all(payload, ("grp_lo",) + VOCAB, 0, 0, tiled=True)
    shard_max, shard_sums, shard_expected, shard_target, shard_root, shard_keep = (
        received[:, k] for k in range(6)
    )
    peak = jnp.max(shard_max, axis=0)
    scale = jnp.exp(shard_max - peak[None, :])
    totals = jnp.sum(shard_sums * scale, axis=0)
    own_expected = jnp.sum(shard_expected * scale, axis=0)
    own_target = jnp.sum(shard_target, axis=0)
    own_root = jnp.sum(shard_root, axis=0)
    keep = jnp.sum(shard_keep, axis=0)
    log_total = jnp.log(totals)
    log_prob = (own_target - peak - log_total) * keep
    entropy = (peak + log_total - own_expected / totals) * keep
    return (log_prob[None], entropy[None], (own_root * keep)[None], (peak * keep)[None])


def solution(mesh):
    vocab_size, group_size = mesh.devices.shape
    assert vocab_size % 2 == 0 and group_size % 2 == 0
    split = Mesh(mesh.devices.reshape(vocab_size // 2, 2, group_size // 2, 2), VOCAB + GROUP)
    in_specs = (
        P(GROUP, VOCAB, None),
        P(GROUP, VOCAB),
        P(GROUP, None),
        P(),
        P(),
        P(None, VOCAB),
    )
    out_specs = (P(GROUP, VOCAB),) * 4
    return jax.shard_map(shards, mesh=split, in_specs=in_specs, out_specs=out_specs, check_vma=False)
```

```python
from functools import partial

import jax
import jax.numpy as jnp
from jax import lax
from jax.experimental import pallas as pl
from jax.sharding import Mesh, PartitionSpec as P

EPSILON = 1e-05
RADIX_BITS = 8
RADIX = 1 << RADIX_BITS
VOCAB = ("vocab_hi", "vocab_lo")
GROUP = ("grp_hi", "grp_lo")
LANES = 128


def digit_count(total):
    digits = 1
    while RADIX**digits < total:
        digits += 1
    return digits


def normalize(block_states, gain):
    values = block_states.astype(jnp.float32)
    mean_square = jnp.mean(values * values, axis=-1)
    normed = (values * lax.rsqrt(mean_square + EPSILON)[:, None] * gain).astype(jnp.bfloat16)
    return (normed, jnp.sqrt(mean_square))


def partial_stats(normed, columns, token_ids, offset):
    logits = jnp.dot(normed, columns, preferred_element_type=jnp.float32)
    local_max = jnp.max(logits, axis=1)
    weights = jnp.exp(logits - local_max[:, None])
    within = token_ids - offset
    column = lax.broadcasted_iota(jnp.int32, logits.shape, 1)
    return (
        local_max,
        jnp.sum(weights, axis=1),
        jnp.sum(weights * logits, axis=1),
        jnp.sum(jnp.where(column == within[:, None], logits, 0.0), axis=1),
    )


def pack_kernel(states_ref, gain_ref, ids_ref, out_ref, *, features, digits):
    values = states_ref[...].astype(jnp.float32)
    mean_square = jnp.mean(values * values, axis=1, keepdims=True)
    normed = (values * lax.rsqrt(mean_square + EPSILON) * gain_ref[...]).astype(jnp.bfloat16)
    out_ref[:, :features] = normed
    ids = ids_ref[...]
    count = ids.shape[1]
    row = lax.broadcasted_iota(jnp.int32, (count, count), 0)
    col = lax.broadcasted_iota(jnp.int32, (count, count), 1)
    token = jnp.sum(jnp.where(row == col, jnp.broadcast_to(ids, (count, count)), 0), axis=1, keepdims=True)
    lane = lax.broadcasted_iota(jnp.int32, (count, LANES), 1)
    code = jnp.zeros((count, LANES), jnp.int32)
    for k in range(digits):
        code = jnp.where(lane == k, (token >> (RADIX_BITS * k)) & (RADIX - 1), code)
    out_ref[:, features:] = code.astype(jnp.float32).astype(jnp.bfloat16)


def pack_rows(block_states, gain, token_ids, digits):
    count, features = block_states.shape
    return pl.pallas_call(
        partial(pack_kernel, features=features, digits=digits),
        out_shape=jax.ShapeDtypeStruct((count, features + LANES), jnp.bfloat16),
    )(block_states, gain.reshape(1, features), token_ids)


def shards(states, target_ids, lengths, order, gain, head):
    count = states.shape[1]
    vocab_size = lax.axis_size(VOCAB)
    group_size = lax.axis_size(GROUP)
    vocab_index = lax.axis_index(VOCAB)
    group_index = lax.axis_index(GROUP)
    core = group_index % 2
    pair_base = group_index - core
    own_order = lax.dynamic_index_in_dim(order, group_index, 0, keepdims=False)
    block_ids = jnp.arange(vocab_size, dtype=jnp.int32)
    root_mean = jnp.sqrt(jnp.mean(jnp.square(states[0].astype(jnp.float32)), axis=-1))
    width = head.shape[1]
    features = states.shape[2]
    digits = digit_count(width * vocab_size)
    place = RADIX ** jnp.arange(digits, dtype=jnp.int32)
    packed = pack_rows(states[0], gain, target_ids, digits)
    low_index = lax.axis_index("vocab_lo")
    if lax.axis_size("vocab_lo") == 2:
        positions = jnp.arange(vocab_size, dtype=jnp.int32)
        block_of = (positions // 2) * 2 + ((positions % 2) ^ low_index)
        received_low = lax.ppermute(packed, "vocab_lo", [(0, 1), (1, 0)])
    else:
        block_of = block_ids
        received_low = packed
    pair_order = lax.dynamic_slice_in_dim(order, pair_base, 2, 0)
    pair_order = jnp.take(pair_order, block_of, axis=1)
    route = (pair_order[:, None, :] == block_ids[None, :, None]).astype(jnp.float32)
    own_length = lax.dynamic_index_in_dim(lengths[0], vocab_index, 0, keepdims=False)
    own_keep = (jnp.arange(count, dtype=jnp.int32) < own_length).astype(jnp.float32)
    route, own_keep, received_low = lax.optimization_barrier((route, own_keep, received_low))
    if lax.axis_size("vocab_lo") == 2:
        packed = jnp.concatenate([packed, received_low])
    else:
        packed = lax.all_gather(packed, "vocab_lo", axis=0, tiled=True)
    packed = lax.all_gather(packed, "vocab_hi", axis=0, tiled=True)
    partner = lax.ppermute(packed, "grp_lo", [(0, 1), (1, 0)])
    pair_rows = jnp.where(core == 0, jnp.concatenate([packed, partner]), jnp.concatenate([partner, packed]))
    pair_normed = pair_rows[:, :features]
    pair_ids = jnp.sum(pair_rows[:, features : features + digits].astype(jnp.int32) * place[None, :], axis=1)
    span = width // 2
    columns = lax.dynamic_slice_in_dim(head, core * span, span, 1)
    offset = vocab_index * width + core * span
    local_max, sums, expected, target = partial_stats(pair_normed, columns, pair_ids, offset)
    at_home = (block_of[:, None] == vocab_index).astype(jnp.float32)
    blank = jnp.zeros((vocab_size, count), jnp.float32)

    def home_term(values):
        own_block = at_home * values[None, :]
        return jnp.where(
            core == 0, jnp.concatenate([own_block, blank]), jnp.concatenate([blank, own_block])
        ).reshape(-1)

    terms = jnp.stack([local_max, sums, expected, target, home_term(root_mean), home_term(own_keep)])
    terms = terms.reshape(6, 2, vocab_size, count)
    routed = jnp.einsum("cjs,kcsr->cjkr", route, terms, precision=lax.Precision.HIGHEST)
    payload = routed.reshape(2 * vocab_size, 6, count)
    received = lax.all_to_all(payload, ("grp_lo",) + VOCAB, 0, 0, tiled=True)
    shard_max, shard_sums, shard_expected, shard_target, shard_root, shard_keep = (
        received[:, k] for k in range(6)
    )
    peak = jnp.max(shard_max, axis=0)
    scale = jnp.exp(shard_max - peak[None, :])
    totals = jnp.sum(shard_sums * scale, axis=0)
    own_expected = jnp.sum(shard_expected * scale, axis=0)
    own_target = jnp.sum(shard_target, axis=0)
    own_root = jnp.sum(shard_root, axis=0)
    keep = jnp.sum(shard_keep, axis=0)
    log_total = jnp.log(totals)
    log_prob = (own_target - peak - log_total) * keep
    entropy = (peak + log_total - own_expected / totals) * keep
    return (log_prob[None], entropy[None], (own_root * keep)[None], (peak * keep)[None])


def solution(mesh):
    vocab_size, group_size = mesh.devices.shape
    assert vocab_size % 2 == 0 and group_size % 2 == 0
    split = Mesh(mesh.devices.reshape(vocab_size // 2, 2, group_size // 2, 2), VOCAB + GROUP)
    in_specs = (
        P(GROUP, VOCAB, None),
        P(GROUP, VOCAB),
        P(GROUP, None),
        P(),
        P(),
        P(None, VOCAB),
    )
    out_specs = (P(GROUP, VOCAB),) * 4
    return jax.shard_map(shards, mesh=split, in_specs=in_specs, out_specs=out_specs, check_vma=False)
```
